512 devices in a mesh: row: 64 (over z, y_lo, core), col: 8 (over y_hi, x).
Axes of the slice: x: 4, y: 4 (y_hi: 2, y_lo: 2; y = y_hi * 2 + y_lo), z: 16, core: 2. Of those that a mesh axis runs over, the one named last changes fastest.
Arguments:
- p_band: bfloat16 [640, 16, 128, 128], P('row', 'col'), may hold values from -6 to 6
- blocks: bfloat16 [640, 3, 128, 128], P('row'), may hold values from -0.375 to 0.375
- block_offsets: int32 [640, 3], P('row'), may hold values from -1 to 1
- block_live: int32 [640], P('row'), may hold values from 1 to 3, as said below
- q_var: float32 [640, 128], P('row'), may hold values from 0.1 to 1
Outputs:
- propagated: bfloat16 [640, 16, 128, 128], P('row', 'col')
The draws below stay inside these ranges and needn't reach their ends.
Inputs may be any that keep to these rules, and one draw needn't show every extreme that they name: `block_live`: tile rows with all 3 blocks live come in runs.
All inputs are finite; a program needn't handle non-finite values.
Results may differ from the reference program's by a relative error of at most 0.0058.
Values may be sent and summed in bfloat16 or wider, within the bound.
No kernel may reach another device: no remote copies, remote signals or barrier semaphores. Data moves between devices by JAX's collectives and lax.ppermute only.
A program may use at most 64 MiB of HBM per device.

```python
import math
import jax
import jax.numpy as jnp
from jax import lax

TS = 128
NB = 16
KA = 3
TILE_ROWS_LOCAL = 10
NT = 640


def draw_block_live(key, part):
    row_ids = jnp.arange(NT, dtype=jnp.int32)
    first_key, second_key, third_key = jax.random.split(key, 3)
    phase_shift = jax.random.randint(first_key, (), 0, 8)
    region = (row_ids + phase_shift) // 8
    dense = jax.random.randint(second_key, (NT // 8 + 2,), 0, 4) == 0
    sparse_count = jax.random.randint(third_key, (NT,), 1, KA)
    counts = jnp.where(dense[region], KA, sparse_count)
    counts = jnp.where(row_ids == 0, KA, counts)
    counts = jnp.where(row_ids == NT - 1, 1, counts)
    return counts.astype(jnp.int32)


def with_ends(drawn, rng, least, top_value):
    longest = drawn.shape.index(max(drawn.shape))
    spots = []
    for shift in (0, 1):
        where = [jax.random.randint(jax.random.fold_in(rng, axis), (), 0, length) for axis, length in enumerate(drawn.shape)]
        where[longest] = (where[longest] + shift) % drawn.shape[longest]
        spots.append(tuple(where))
    return drawn.at[spots[0]].set(least).at[spots[1]].set(top_value)


def levels(rng, dims, cuts, least, top_value):
    loudness, own = 1.0, jax.random.fold_in(rng, 6)
    for axis_at, shards_of in cuts:
        heights = jnp.exp(jax.random.uniform(jax.random.fold_in(own, axis_at), (shards_of,), jnp.float32, least / len(cuts), top_value / len(cuts)))
        loudness = loudness * jnp.repeat(heights, dims[axis_at] // shards_of).reshape([-1 if axis == axis_at else 1 for axis in range(len(dims))])
    return loudness


def scatter_about(key, extent, spread, limit, cuts=(), kind=jnp.bfloat16):
    array = spread * jax.random.normal(key, extent, jnp.float32)
    if cuts:
        array = array * levels(key, extent, cuts, -0.22, 0.18)
    return jnp.clip(array, -limit, limit).astype(kind)


def setup_inputs(seed: int = 0) -> dict:
    splits = jax.random.split(jax.random.key(seed), 6)
    p_band = scatter_about(splits[0], (NT, NB, TS, TS), 1.0, 6.0, ((0, 64), (1, 8)))
    blocks = scatter_about(splits[1], (NT, KA, TS, TS), (2 * TS) ** -0.5, 0.375, ((0, 64),))
    block_offsets = with_ends(jax.random.randint(splits[2], (NT, KA), -1, 2), jax.random.fold_in(splits[2], 1), -1, 1).astype(jnp.int32)
    block_live = draw_block_live(jax.random.fold_in(splits[5], 71), 0)
    q_var = jnp.clip(jnp.exp(math.log(1.0) - 2.3025851 * jax.random.uniform(splits[4], (NT, TS), jnp.float32) ** levels(splits[4], (NT, TS), ((0, 64),), -0.2, 0.2)), 0.1, 1.0)
    return dict(p_band=p_band, blocks=blocks, block_offsets=block_offsets, block_live=block_live, q_var=q_var)


def assemble(blocks, block_offsets, block_live):
    slot_ids = jnp.arange(blocks.shape[1], dtype=jnp.int32)
    alive = slot_ids[None, :] < block_live[:, None]
    targets = jnp.arange(3, dtype=jnp.int32) - 1
    choose = (block_offsets[:, :, None] == targets[None, None, :]) & alive[:, :, None]
    summed_total = jnp.einsum("tmf,tmab->tfab", choose.astype(jnp.float32), blocks.astype(jnp.float32))
    return summed_total.astype(jnp.bfloat16)


def reference(p_band, blocks, block_offsets, block_live, q_var):
    half_band = NB // 2
    row_ids = jnp.arange(NT, dtype=jnp.int32)[:, None]
    columns = row_ids + jnp.arange(NB, dtype=jnp.int32)[None, :] - half_band
    inside = (columns >= 0) & (columns < NT)
    prior = jnp.where(inside[:, :, None, None], p_band, jnp.zeros_like(p_band))
    jacobian = assemble(blocks, block_offsets, block_live)
    padded = jnp.pad(prior, ((1, 1), (2, 2), (0, 0), (0, 0)))
    jacobian_extended_rows = jnp.pad(jacobian, ((half_band, half_band), (0, 0), (0, 0), (0, 0)))
    eye_tile = jnp.eye(TS, dtype=jnp.float32)

    def single_block_piece(begin):
        prow_block = lax.dynamic_slice_in_dim(padded, begin, TILE_ROWS_LOCAL + 2, 0)
        jrow_block = lax.dynamic_slice_in_dim(jacobian, begin, TILE_ROWS_LOCAL, 0)
        spread_sum = jnp.zeros((TILE_ROWS_LOCAL, NB + 2, TS, TS), jnp.float32)
        for shift_f in range(3):
            source = prow_block[shift_f:shift_f + TILE_ROWS_LOCAL, 2 - shift_f:2 - shift_f + NB + 2].astype(jnp.float32)
            spread_sum = spread_sum + jnp.einsum("tab,tubc->tuac", jrow_block[:, shift_f].astype(jnp.float32), source)
        spread_out_block = spread_sum.astype(jnp.bfloat16)
        window_slice = lax.dynamic_slice_in_dim(jacobian_extended_rows, begin, TILE_ROWS_LOCAL + NB - 1, 0)
        noise_rows = lax.dynamic_slice_in_dim(q_var, begin, TILE_ROWS_LOCAL, 0)
        results = []
        for offset_position in range(NB):
            summed_total = jnp.zeros((TILE_ROWS_LOCAL, TS, TS), jnp.float32)
            for shift_amount_second in range(3):
                summed_total = summed_total + jnp.einsum("kmg,kvg->kmv", spread_out_block[:, offset_position + shift_amount_second].astype(jnp.float32), window_slice[offset_position:offset_position + TILE_ROWS_LOCAL, shift_amount_second].astype(jnp.float32))
            if offset_position == half_band:
                summed_total = summed_total + noise_rows[:, :, None] * eye_tile[None]
            results.append(summed_total)
        return jnp.stack(results, axis=1)

    begins = jnp.arange(NT // TILE_ROWS_LOCAL, dtype=jnp.int32) * TILE_ROWS_LOCAL
    block_out = lax.map(single_block_piece, begins)
    result = block_out.reshape(NT, NB, TS, TS)
    return jnp.where(inside[:, :, None, None], result, jnp.zeros_like(result)).astype(jnp.bfloat16)
```

```python
import jax
import jax.numpy as jnp
from jax import lax
from jax.sharding import PartitionSpec as P


def assemble(blocks, block_offsets, block_live):
    slot_ids = jnp.arange(blocks.shape[1], dtype=jnp.int32)
    alive = slot_ids[None, :] < block_live[:, None]
    targets = jnp.arange(3, dtype=jnp.int32) - 1
    choose = (block_offsets[:, :, None] == targets[None, None, :]) & alive[:, :, None]
    summed_total = jnp.einsum(
        "tmf,tmab->tfab", choose.astype(jnp.bfloat16), blocks, preferred_element_type=jnp.float32
    )
    return summed_total.astype(jnp.bfloat16)


def tile_product(form, operand_one, operand_two):
    batched = "t" + form.replace(",", ",t").replace(">", ">t")
    return jnp.einsum(batched, operand_one, operand_two, preferred_element_type=jnp.float32)


def shards(p_band, blocks, block_offsets, block_live, q_var):
    tile_rows, band_local, tile_size = p_band.shape[0], p_band.shape[1], p_band.shape[2]
    row_count = lax.axis_size("row")
    col_count = lax.axis_size("col")
    half_band = band_local * col_count // 2
    grid_tiles = tile_rows * row_count
    row_id = lax.axis_index("row")
    col_id = lax.axis_index("col")
    first_row = row_id * tile_rows
    low_offset = col_id * band_local - half_band
    row_ids = first_row + jnp.arange(tile_rows, dtype=jnp.int32)[:, None]
    columns = row_ids + low_offset + jnp.arange(band_local, dtype=jnp.int32)[None, :]
    inside = (columns >= 0) & (columns < grid_tiles)
    prior = jnp.where(inside[:, :, None, None], p_band, jnp.zeros_like(p_band))
    jacobian = assemble(blocks, block_offsets, block_live)

    def flat(a, b):
        return a * col_count + b

    left = lax.ppermute(prior, "col", [(b, b + 1) for b in range(col_count - 1)])
    right = lax.ppermute(prior, "col", [(b + 1, b) for b in range(col_count - 1)])
    up = lax.ppermute(prior[-1], "row", [(a, a + 1) for a in range(row_count - 1)])
    down = lax.ppermute(prior[0], "row", [(a + 1, a) for a in range(row_count - 1)])
    up_right = lax.ppermute(
        prior[-1],
        ("row", "col"),
        [(flat(a, b), flat(a + 1, b - 1)) for a in range(row_count - 1) for b in range(1, col_count)],
    )
    down_left = lax.ppermute(
        prior[0],
        ("row", "col"),
        [(flat(a, b), flat(a - 1, b + 1)) for a in range(1, row_count) for b in range(col_count - 1)],
    )

    window = tile_rows + band_local - 1
    sent_rows = half_band
    lower_half = col_id < col_count // 2
    send_start = jnp.where(lower_half, tile_rows - sent_rows, 0)
    sent = lax.dynamic_slice_in_dim(jacobian, send_start, sent_rows, 0)
    pairs = []
    for b in range(col_count):
        if b * band_local - half_band < 0:
            pairs += [(flat(a, b), flat(a + 1, b)) for a in range(row_count - 1)]
        else:
            pairs += [(flat(a, b), flat(a - 1, b)) for a in range(1, row_count)]
    received = lax.ppermute(sent, ("row", "col"), pairs)
    extended_rows = jnp.concatenate([received, jacobian, received], axis=0)
    window_slice = lax.dynamic_slice_in_dim(extended_rows, sent_rows + low_offset, window, 0)

    zero_pair = jnp.zeros((2, tile_size, tile_size), prior.dtype)
    middle = jnp.concatenate([left[:, band_local - 2 :], prior, right[:, :2]], axis=1)
    top = jnp.concatenate([zero_pair, up, up_right[:2]], axis=0)
    bottom = jnp.concatenate([down_left[band_local - 2 :], down, zero_pair], axis=0)
    padded = jnp.concatenate([top[None], middle, bottom[None]], axis=0)

    extended = band_local + 2
    spread_sum = jnp.zeros((tile_rows, extended, tile_size, tile_size), jnp.float32)
    for shift_f in range(3):
        source = padded[shift_f : shift_f + tile_rows, 2 - shift_f : 2 - shift_f + extended]
        spread_sum = spread_sum + tile_product("ab,ubc->uac", jacobian[:, shift_f], source)
    spread_out_block = spread_sum.astype(jnp.bfloat16)

    eye_tile = jnp.eye(tile_size, dtype=jnp.float32)
    noise = q_var[:, :, None] * eye_tile[None]
    tile_shape = (tile_rows, tile_size, tile_size)
    results = []
    for offset_position in range(band_local):
        summed_total = jnp.zeros(tile_shape, jnp.float32)
        for shift_amount_second in range(3):
            summed_total = summed_total + tile_product(
                "ab,cb->ac",
                spread_out_block[:, offset_position + shift_amount_second],
                window_slice[offset_position : offset_position + tile_rows, shift_amount_second],
            )
        on_diagonal = low_offset + offset_position == 0
        summed_total = summed_total + jnp.where(on_diagonal, noise, jnp.zeros_like(noise))
        results.append(summed_total)
    stacked = jnp.stack(results, axis=1)
    return jnp.where(inside[:, :, None, None], stacked, jnp.zeros_like(stacked)).astype(
        jnp.bfloat16
    )


def solution(mesh):
    placed = (
        P("row", "col", None, None),
        P("row", None, None, None),
        P("row", None),
        P("row"),
        P("row", None),
    )
    return jax.shard_map(
        shards, mesh=mesh, in_specs=placed, out_specs=P("row", "col", None, None), check_vma=False
    )
```

```python
import jax
import jax.numpy as jnp
from jax import lax
from jax.experimental import pallas as pl
from jax.experimental.pallas import tpu as pltpu
from jax.sharding import PartitionSpec as P


def assemble(blocks, block_offsets, block_live):
    slot_ids = jnp.arange(blocks.shape[1], dtype=jnp.int32)
    alive = slot_ids[None, :] < block_live[:, None]
    pieces = []
    for target in (-1, 0, 1):
        choose = (block_offsets == target) & alive
        total = jnp.zeros(blocks.shape[:1] + blocks.shape[2:], jnp.float32)
        for m in range(blocks.shape[1]):
            total = total + jnp.where(choose[:, m, None, None], blocks[:, m].astype(jnp.float32), 0.0)
        pieces.append(total.astype(jnp.bfloat16))
    return jnp.stack(pieces, axis=1)


def band_kernel(tile_rows, band_local, half_band, grid_tiles):
    extended = band_local + 2

    def kernel(ids, q_ref, jac_ref, win_ref, mid_ref, left_ref, right_ref, top_ref, bot_ref, out_ref):
        row_id = ids[0]
        col_id = ids[1]
        first_row = row_id * tile_rows
        low_slot = col_id * band_local - 2
        size = jac_ref.shape[-1]

        def prior_tile(ext_row, ext_slot):
            if ext_row == 0:
                tile = top_ref[ext_slot]
            elif ext_row == tile_rows + 1:
                tile = bot_ref[ext_slot]
            elif ext_slot < 2:
                tile = left_ref[ext_row - 1, band_local - 2 + ext_slot]
            elif ext_slot < 2 + band_local:
                tile = mid_ref[ext_row - 1, ext_slot - 2]
            else:
                tile = right_ref[ext_row - 1, ext_slot - 2 - band_local]
            column = first_row + ext_row - 1 + low_slot + ext_slot - half_band
            keep = (column >= 0) & (column < grid_tiles)
            return jnp.where(keep, tile, jnp.zeros_like(tile))

        eye = lax.broadcasted_iota(jnp.int32, (size, size), 0) == lax.broadcasted_iota(
            jnp.int32, (size, size), 1
        )
        for row in range(tile_rows):
            lhs = jnp.concatenate([jac_ref[row, f] for f in range(3)], axis=1)
            rhs = jnp.concatenate(
                [
                    jnp.concatenate(
                        [prior_tile(row + f, u - f + 2) for u in range(extended)], axis=1
                    )
                    for f in range(3)
                ],
                axis=0,
            )
            spread = jnp.dot(lhs, rhs, preferred_element_type=jnp.float32).astype(jnp.bfloat16)
            for k in range(band_local):
                left_side = spread[:, k * size : (k + 3) * size]
                right_side = jnp.concatenate([win_ref[row + k, g] for g in range(3)], axis=1)
                total = lax.dot_general(
                    left_side,
                    right_side,
                    (((1,), (1,)), ((), ())),
                    preferred_element_type=jnp.float32,
                )
                on_diagonal = col_id * band_local + k == half_band
                noise = jnp.where(eye & on_diagonal, q_ref[pl.ds(row, 1), :], 0.0)
                total = total + noise
                column = first_row + row + col_id * band_local + k - half_band
                keep = (column >= 0) & (column < grid_tiles)
                total = jnp.where(keep, total, jnp.zeros_like(total))
                out_ref[row, k] = total.astype(out_ref.dtype)

    return kernel


def shards(p_band, blocks, block_offsets, block_live, q_var):
    tile_rows, band_local, tile_size = p_band.shape[0], p_band.shape[1], p_band.shape[2]
    row_count = lax.axis_size("row")
    col_count = lax.axis_size("col")
    half_band = band_local * col_count // 2
    grid_tiles = tile_rows * row_count
    row_id = lax.axis_index("row")
    col_id = lax.axis_index("col")
    low_offset = col_id * band_local - half_band

    def flat(a, b):
        return a * col_count + b

    left = lax.ppermute(p_band, "col", [(b, b + 1) for b in range(col_count - 1)])
    right = lax.ppermute(p_band, "col", [(b + 1, b) for b in range(col_count - 1)])
    up = lax.ppermute(p_band[-1], "row", [(a, a + 1) for a in range(row_count - 1)])
    down = lax.ppermute(p_band[0], "row", [(a + 1, a) for a in range(row_count - 1)])
    up_right = lax.ppermute(
        p_band[-1],
        ("row", "col"),
        [(flat(a, b), flat(a + 1, b - 1)) for a in range(row_count - 1) for b in range(1, col_count)],
    )
    down_left = lax.ppermute(
        p_band[0],
        ("row", "col"),
        [(flat(a, b), flat(a - 1, b + 1)) for a in range(1, row_count) for b in range(col_count - 1)],
    )

    jacobian = assemble(blocks, block_offsets, block_live)

    window = tile_rows + band_local - 1
    sent_rows = half_band
    lower_half = col_id < col_count // 2
    send_start = jnp.where(lower_half, tile_rows - sent_rows, 0)
    sent = lax.dynamic_slice_in_dim(jacobian, send_start, sent_rows, 0)
    pairs = []
    for b in range(col_count):
        if b * band_local - half_band < 0:
            pairs += [(flat(a, b), flat(a + 1, b)) for a in range(row_count - 1)]
        else:
            pairs += [(flat(a, b), flat(a - 1, b)) for a in range(1, row_count)]
    received = lax.ppermute(sent, ("row", "col"), pairs)
    extended_rows = jnp.concatenate([received, jacobian, received], axis=0)
    window_slice = lax.dynamic_slice_in_dim(extended_rows, sent_rows + low_offset, window, 0)

    zero_pair = jnp.zeros((2, tile_size, tile_size), p_band.dtype)
    top = jnp.concatenate([zero_pair, up, up_right[:2]], axis=0)
    bottom = jnp.concatenate([down_left[band_local - 2 :], down, zero_pair], axis=0)

    ids = jnp.stack([row_id, col_id]).astype(jnp.int32)
    vmem = pl.BlockSpec(memory_space=pltpu.MemorySpace.VMEM)
    smem = pl.BlockSpec(memory_space=pltpu.MemorySpace.SMEM)
    return pl.pallas_call(
        band_kernel(tile_rows, band_local, half_band, grid_tiles),
        out_shape=jax.ShapeDtypeStruct(p_band.shape, p_band.dtype),
        in_specs=[smem] + [vmem] * 8,
        out_specs=vmem,
    )(ids, q_var, jacobian, window_slice, p_band, left, right, top, bottom)


def solution(mesh):
    placed = (
        P("row", "col", None, None),
        P("row", None, None, None),
        P("row", None),
        P("row"),
        P("row", None),
    )
    return jax.shard_map(
        shards, mesh=mesh, in_specs=placed, out_specs=P("row", "col", None, None), check_vma=False
    )
```

```python
import jax
import jax.numpy as jnp
from jax import lax
from jax.experimental import pallas as pl
from jax.experimental.pallas import tpu as pltpu
from jax.sharding import PartitionSpec as P


def assemble(blocks, block_offsets, block_live):
    slot_ids = jnp.arange(blocks.shape[1], dtype=jnp.int32)
    alive = slot_ids[None, :] < block_live[:, None]
    pieces = []
    for target in (-1, 0, 1):
        choose = (block_offsets == target) & alive
        total = jnp.zeros(blocks.shape[:1] + blocks.shape[2:], jnp.float32)
        for m in range(blocks.shape[1]):
            total = total + jnp.where(choose[:, m, None, None], blocks[:, m].astype(jnp.float32), 0.0)
        pieces.append(total.astype(jnp.bfloat16))
    return jnp.stack(pieces, axis=1)


def band_kernel(tile_rows, band_local, half_band, grid_tiles, sent_rows):
    extended = band_local + 2

    def kernel(ids, q_ref, jac_ref, recv_ref, mid_ref, left_ref, right_ref, up_ref, up_right_ref,
               down_ref, down_left_ref, out_ref):
        row_id = ids[0]
        col_id = ids[1]
        first_row = row_id * tile_rows
        low_slot = col_id * band_local - 2
        low_offset = col_id * band_local - half_band
        size = jac_ref.shape[-1]

        def prior_tile(ext_row, ext_slot):
            if ext_row == 0:
                if ext_slot < 2 + band_local:
                    tile = up_ref[ext_slot - 2]
                else:
                    tile = up_right_ref[ext_slot - 2 - band_local]
            elif ext_row == tile_rows + 1:
                if ext_slot < 2:
                    tile = down_left_ref[band_local - 2 + ext_slot]
                else:
                    tile = down_ref[ext_slot - 2]
            elif ext_slot < 2:
                tile = left_ref[ext_row - 1, band_local - 2 + ext_slot]
            elif ext_slot < 2 + band_local:
                tile = mid_ref[ext_row - 1, ext_slot - 2]
            else:
                tile = right_ref[ext_row - 1, ext_slot - 2 - band_local]
            column = first_row + ext_row - 1 + low_slot + ext_slot - half_band
            keep = (column >= 0) & (column < grid_tiles)
            return jnp.where(keep, tile, jnp.zeros_like(tile))

        def window_tile(position, g):
            at = sent_rows + low_offset + position
            before = recv_ref[jnp.clip(at, 0, sent_rows - 1), g]
            own = jac_ref[jnp.clip(at - sent_rows, 0, tile_rows - 1), g]
            after = recv_ref[jnp.clip(at - sent_rows - tile_rows, 0, sent_rows - 1), g]
            return jnp.where(at < sent_rows, before, jnp.where(at < sent_rows + tile_rows, own, after))

        eye = lax.broadcasted_iota(jnp.int32, (size, size), 0) == lax.broadcasted_iota(
            jnp.int32, (size, size), 1
        )
        for row in range(tile_rows):
            lhs = jnp.concatenate([jac_ref[row, f] for f in range(3)], axis=1)
            rhs = jnp.concatenate(
                [
                    jnp.concatenate(
                        [prior_tile(row + f, u - f + 2) for u in range(extended)], axis=1
                    )
                    for f in range(3)
                ],
                axis=0,
            )
            spread = jnp.dot(lhs, rhs, preferred_element_type=jnp.float32).astype(jnp.bfloat16)
            for k in range(band_local):
                left_side = spread[:, k * size : (k + 3) * size]
                right_side = jnp.concatenate([window_tile(row + k, g) for g in range(3)], axis=1)
                total = lax.dot_general(
                    left_side,
                    right_side,
                    (((1,), (1,)), ((), ())),
                    preferred_element_type=jnp.float32,
                )
                on_diagonal = low_offset + k == 0
                noise = jnp.where(eye & on_diagonal, q_ref[pl.ds(row, 1), :], 0.0)
                total = total + noise
                column = first_row + row + low_offset + k
                keep = (column >= 0) & (column < grid_tiles)
                total = jnp.where(keep, total, jnp.zeros_like(total))
                out_ref[row, k] = total.astype(out_ref.dtype)

    return kernel


def shards(p_band, blocks, block_offsets, block_live, q_var):
    tile_rows, band_local, tile_size = p_band.shape[0], p_band.shape[1], p_band.shape[2]
    row_count = lax.axis_size("row")
    col_count = lax.axis_size("col")
    half_band = band_local * col_count // 2
    grid_tiles = tile_rows * row_count
    row_id = lax.axis_index("row")
    col_id = lax.axis_index("col")
    low_offset = col_id * band_local - half_band

    def flat(a, b):
        return a * col_count + b

    left = lax.ppermute(p_band, "col", [(b, b + 1) for b in range(col_count - 1)])
    right = lax.ppermute(p_band, "col", [(b + 1, b) for b in range(col_count - 1)])
    up = lax.ppermute(p_band[-1], "row", [(a, a + 1) for a in range(row_count - 1)])
    down = lax.ppermute(p_band[0], "row", [(a + 1, a) for a in range(row_count - 1)])
    up_right = lax.ppermute(
        p_band[-1],
        ("row", "col"),
        [(flat(a, b), flat(a + 1, b - 1)) for a in range(row_count - 1) for b in range(1, col_count)],
    )
    down_left = lax.ppermute(
        p_band[0],
        ("row", "col"),
        [(flat(a, b), flat(a - 1, b + 1)) for a in range(1, row_count) for b in range(col_count - 1)],
    )

    jacobian = assemble(blocks, block_offsets, block_live)

    sent_rows = half_band
    lower_half = col_id < col_count // 2
    send_start = jnp.where(lower_half, tile_rows - sent_rows, 0)
    sent = lax.dynamic_slice_in_dim(jacobian, send_start, sent_rows, 0)
    pairs = []
    for b in range(col_count):
        if b * band_local - half_band < 0:
            pairs += [(flat(a, b), flat(a + 1, b)) for a in range(row_count - 1)]
        else:
            pairs += [(flat(a, b), flat(a - 1, b)) for a in range(1, row_count)]
    received = lax.ppermute(sent, ("row", "col"), pairs)

    ids = jnp.stack([row_id, col_id]).astype(jnp.int32)
    vmem = pl.BlockSpec(memory_space=pltpu.MemorySpace.VMEM)
    smem = pl.BlockSpec(memory_space=pltpu.MemorySpace.SMEM)
    return pl.pallas_call(
        band_kernel(tile_rows, band_local, half_band, grid_tiles, sent_rows),
        out_shape=jax.ShapeDtypeStruct(p_band.shape, p_band.dtype),
        in_specs=[smem] + [vmem] * 10,
        out_specs=vmem,
    )(ids, q_var, jacobian, received, p_band, left, right, up, up_right, down, down_left)


def solution(mesh):
    placed = (
        P("row", "col", None, None),
        P("row", None, None, None),
        P("row", None),
        P("row"),
        P("row", None),
    )
    return jax.shard_map(
        shards, mesh=mesh, in_specs=placed, out_specs=P("row", "col", None, None), check_vma=False
    )
```

```python
import jax
import jax.numpy as jnp
from jax import lax
from jax.experimental import pallas as pl
from jax.experimental.pallas import tpu as pltpu
from jax.sharding import PartitionSpec as P


def assemble(blocks, block_offsets, block_live):
    slot_ids = jnp.arange(blocks.shape[1], dtype=jnp.int32)
    alive = slot_ids[None, :] < block_live[:, None]
    pieces = []
    for target in (-1, 0, 1):
        choose = (block_offsets == target) & alive
        total = jnp.zeros(blocks.shape[:1] + blocks.shape[2:], jnp.float32)
        for m in range(blocks.shape[1]):
            total = total + jnp.where(choose[:, m, None, None], blocks[:, m].astype(jnp.float32), 0.0)
        pieces.append(total.astype(jnp.bfloat16))
    return jnp.stack(pieces, axis=1)


def band_kernel(tile_rows, band_local, half_band, grid_tiles, sent_rows):
    extended = band_local + 2

    def kernel(ids, q_ref, jac_ref, recv_ref, mid_ref, left_ref, right_ref, up_ref, down_ref, out_ref):
        row_id = ids[0]
        col_id = ids[1]
        first_row = row_id * tile_rows
        low_slot = col_id * band_local - 2
        low_offset = col_id * band_local - half_band
        size = jac_ref.shape[-1]

        def prior_tile(ext_row, ext_slot):
            if ext_slot < 2:
                tile = left_ref[ext_row - 1, band_local - 2 + ext_slot]
            elif ext_slot >= 2 + band_local:
                tile = right_ref[ext_row, ext_slot - 2 - band_local]
            elif ext_row == 0:
                tile = up_ref[ext_slot - 2]
            elif ext_row == tile_rows + 1:
                tile = down_ref[ext_slot - 2]
            else:
                tile = mid_ref[ext_row - 1, ext_slot - 2]
            column = first_row + ext_row - 1 + low_slot + ext_slot - half_band
            keep = (column >= 0) & (column < grid_tiles)
            return jnp.where(keep, tile, jnp.zeros_like(tile))

        def window_tile(position, g):
            at = sent_rows + low_offset + position
            before = recv_ref[jnp.clip(at, 0, sent_rows - 1), g]
            own = jac_ref[jnp.clip(at - sent_rows, 0, tile_rows - 1), g]
            after = recv_ref[jnp.clip(at - sent_rows - tile_rows, 0, sent_rows - 1), g]
            return jnp.where(at < sent_rows, before, jnp.where(at < sent_rows + tile_rows, own, after))

        eye = lax.broadcasted_iota(jnp.int32, (size, size), 0) == lax.broadcasted_iota(
            jnp.int32, (size, size), 1
        )
        for row in range(tile_rows):
            lhs = jnp.concatenate([jac_ref[row, f] for f in range(3)], axis=1)
            rhs = jnp.concatenate(
                [
                    jnp.concatenate(
                        [prior_tile(row + f, u - f + 2) for u in range(extended)], axis=1
                    )
                    for f in range(3)
                ],
                axis=0,
            )
            spread = jnp.dot(lhs, rhs, preferred_element_type=jnp.float32).astype(jnp.bfloat16)
            for k in range(band_local):
                left_side = spread[:, k * size : (k + 3) * size]
                right_side = jnp.concatenate([window_tile(row + k, g) for g in range(3)], axis=1)
                total = lax.dot_general(
                    left_side,
                    right_side,
                    (((1,), (1,)), ((), ())),
                    preferred_element_type=jnp.float32,
                )
                on_diagonal = low_offset + k == 0
                noise = jnp.where(eye & on_diagonal, q_ref[pl.ds(row, 1), :], 0.0)
                total = total + noise
                column = first_row + row + low_offset + k
                keep = (column >= 0) & (column < grid_tiles)
                total = jnp.where(keep, total, jnp.zeros_like(total))
                out_ref[row, k] = total.astype(out_ref.dtype)

    return kernel


def shards(p_band, blocks, block_offsets, block_live, q_var):
    tile_rows, band_local, tile_size = p_band.shape[0], p_band.shape[1], p_band.shape[2]
    row_count = lax.axis_size("row")
    col_count = lax.axis_size("col")
    half_band = band_local * col_count // 2
    grid_tiles = tile_rows * row_count
    row_id = lax.axis_index("row")
    col_id = lax.axis_index("col")
    low_offset = col_id * band_local - half_band

    def flat(a, b):
        return a * col_count + b

    up = lax.ppermute(p_band[-1], "row", [(a, a + 1) for a in range(row_count - 1)])
    down = lax.ppermute(p_band[0], "row", [(a + 1, a) for a in range(row_count - 1)])

    jacobian = assemble(blocks, block_offsets, block_live)

    sent_rows = half_band
    lower_half = col_id < col_count // 2
    send_start = jnp.where(lower_half, tile_rows - sent_rows, 0)
    sent = lax.dynamic_slice_in_dim(jacobian, send_start, sent_rows, 0)
    pairs = []
    for b in range(col_count):
        if b * band_local - half_band < 0:
            pairs += [(flat(a, b), flat(a + 1, b)) for a in range(row_count - 1)]
        else:
            pairs += [(flat(a, b), flat(a - 1, b)) for a in range(1, row_count)]
    received = lax.ppermute(sent, ("row", "col"), pairs)

    left_payload = jnp.concatenate([p_band, down[None]], axis=0)
    right_payload = jnp.concatenate([up[None], p_band], axis=0)
    left = lax.ppermute(left_payload, "col", [(b, b + 1) for b in range(col_count - 1)])
    right = lax.ppermute(right_payload, "col", [(b + 1, b) for b in range(col_count - 1)])

    ids = jnp.stack([row_id, col_id]).astype(jnp.int32)
    vmem = pl.BlockSpec(memory_space=pltpu.MemorySpace.VMEM)
    smem = pl.BlockSpec(memory_space=pltpu.MemorySpace.SMEM)
    return pl.pallas_call(
        band_kernel(tile_rows, band_local, half_band, grid_tiles, sent_rows),
        out_shape=jax.ShapeDtypeStruct(p_band.shape, p_band.dtype),
        in_specs=[smem] + [vmem] * 8,
        out_specs=vmem,
    )(ids, q_var, jacobian, received, p_band, left, right, up, down)


def solution(mesh):
    placed = (
        P("row", "col", None, None),
        P("row", None, None, None),
        P("row", None),
        P("row"),
        P("row", None),
    )
    return jax.shard_map(
        shards, mesh=mesh, in_specs=placed, out_specs=P("row", "col", None, None), check_vma=False
    )
```

```python
import jax
import jax.numpy as jnp
from jax import lax
from jax.experimental import pallas as pl
from jax.experimental.pallas import tpu as pltpu
from jax.sharding import PartitionSpec as P


def assemble(blocks, block_offsets, block_live):
    slot_ids = jnp.arange(blocks.shape[1], dtype=jnp.int32)
    alive = slot_ids[None, :] < block_live[:, None]
    pieces = []
    for target in (-1, 0, 1):
        choose = (block_offsets == target) & alive
        total = jnp.zeros(blocks.shape[:1] + blocks.shape[2:], jnp.float32)
        for m in range(blocks.shape[1]):
            total = total + jnp.where(choose[:, m, None, None], blocks[:, m].astype(jnp.float32), 0.0)
        pieces.append(total.astype(jnp.bfloat16))
    return jnp.stack(pieces, axis=1)


def band_kernel(tile_rows, band_local, half_band, grid_tiles, sent_rows):
    extended = band_local + 2

    def kernel(ids, q_ref, jac_ref, recv_ref, mid_ref, left_ref, right_ref, up_ref, down_ref,
               up_right_ref, down_left_ref, out_ref):
        row_id = ids[0]
        col_id = ids[1]
        first_row = row_id * tile_rows
        low_slot = col_id * band_local - 2
        low_offset = col_id * band_local - half_band
        size = jac_ref.shape[-1]

        def prior_tile(ext_row, ext_slot):
            if ext_slot < 2:
                if ext_row == tile_rows + 1:
                    tile = down_left_ref[band_local - 2 + ext_slot]
                else:
                    tile = left_ref[ext_row - 1, band_local - 2 + ext_slot]
            elif ext_slot >= 2 + band_local:
                if ext_row == 0:
                    tile = up_right_ref[ext_slot - 2 - band_local]
                else:
                    tile = right_ref[ext_row - 1, ext_slot - 2 - band_local]
            elif ext_row == 0:
                tile = up_ref[ext_slot - 2]
            elif ext_row == tile_rows + 1:
                tile = down_ref[ext_slot - 2]
            else:
                tile = mid_ref[ext_row - 1, ext_slot - 2]
            column = first_row + ext_row - 1 + low_slot + ext_slot - half_band
            keep = (column >= 0) & (column < grid_tiles)
            return jnp.where(keep, tile, jnp.zeros_like(tile))

        def window_tile(position, g):
            at = sent_rows + low_offset + position
            before = recv_ref[jnp.clip(at, 0, sent_rows - 1), g]
            own = jac_ref[jnp.clip(at - sent_rows, 0, tile_rows - 1), g]
            after = recv_ref[jnp.clip(at - sent_rows - tile_rows, 0, sent_rows - 1), g]
            return jnp.where(at < sent_rows, before, jnp.where(at < sent_rows + tile_rows, own, after))

        eye = lax.broadcasted_iota(jnp.int32, (size, size), 0) == lax.broadcasted_iota(
            jnp.int32, (size, size), 1
        )
        for row in range(tile_rows):
            lhs = jnp.concatenate([jac_ref[row, f] for f in range(3)], axis=1)
            rhs = jnp.concatenate(
                [
                    jnp.concatenate(
                        [prior_tile(row + f, u - f + 2) for u in range(extended)], axis=1
                    )
                    for f in range(3)
                ],
                axis=0,
            )
            spread = jnp.dot(lhs, rhs, preferred_element_type=jnp.float32).astype(jnp.bfloat16)
            for k in range(band_local):
                left_side = spread[:, k * size : (k + 3) * size]
                right_side = jnp.concatenate([window_tile(row + k, g) for g in range(3)], axis=1)
                total = lax.dot_general(
                    left_side,
                    right_side,
                    (((1,), (1,)), ((), ())),
                    preferred_element_type=jnp.float32,
                )
                on_diagonal = low_offset + k == 0
                noise = jnp.where(eye & on_diagonal, q_ref[pl.ds(row, 1), :], 0.0)
                total = total + noise
                column = first_row + row + low_offset + k
                keep = (column >= 0) & (column < grid_tiles)
                total = jnp.where(keep, total, jnp.zeros_like(total))
                out_ref[row, k] = total.astype(out_ref.dtype)

    return kernel


def shards(p_band, blocks, block_offsets, block_live, q_var):
    tile_rows, band_local, tile_size = p_band.shape[0], p_band.shape[1], p_band.shape[2]
    row_count = lax.axis_size("row")
    col_count = lax.axis_size("col")
    half_band = band_local * col_count // 2
    grid_tiles = tile_rows * row_count
    row_id = lax.axis_index("row")
    col_id = lax.axis_index("col")
    low_offset = col_id * band_local - half_band

    def flat(a, b):
        return a * col_count + b

    left = lax.ppermute(p_band, "col", [(b, b + 1) for b in range(col_count - 1)])
    right = lax.ppermute(p_band, "col", [(b + 1, b) for b in range(col_count - 1)])
    up = lax.ppermute(p_band[-1], "row", [(a, a + 1) for a in range(row_count - 1)])
    down = lax.ppermute(p_band[0], "row", [(a + 1, a) for a in range(row_count - 1)])

    jacobian = assemble(blocks, block_offsets, block_live)

    sent_rows = half_band
    lower_half = col_id < col_count // 2
    send_start = jnp.where(lower_half, tile_rows - sent_rows, 0)
    sent = lax.dynamic_slice_in_dim(jacobian, send_start, sent_rows, 0)
    pairs = []
    for b in range(col_count):
        if b * band_local - half_band < 0:
            pairs += [(flat(a, b), flat(a + 1, b)) for a in range(row_count - 1)]
        else:
            pairs += [(flat(a, b), flat(a - 1, b)) for a in range(1, row_count)]
    received = lax.ppermute(sent, ("row", "col"), pairs)

    down_left = lax.ppermute(down, "col", [(b, b + 1) for b in range(col_count - 1)])
    up_right = lax.ppermute(up, "col", [(b + 1, b) for b in range(col_count - 1)])

    ids = jnp.stack([row_id, col_id]).astype(jnp.int32)
    vmem = pl.BlockSpec(memory_space=pltpu.MemorySpace.VMEM)
    smem = pl.BlockSpec(memory_space=pltpu.MemorySpace.SMEM)
    return pl.pallas_call(
        band_kernel(tile_rows, band_local, half_band, grid_tiles, sent_rows),
        out_shape=jax.ShapeDtypeStruct(p_band.shape, p_band.dtype),
        in_specs=[smem] + [vmem] * 10,
        out_specs=vmem,
    )(ids, q_var, jacobian, received, p_band, left, right, up, down, up_right, down_left)


def solution(mesh):
    placed = (
        P("row", "col", None, None),
        P("row", None, None, None),
        P("row", None),
        P("row"),
        P("row", None),
    )
    return jax.shard_map(
        shards, mesh=mesh, in_specs=placed, out_specs=P("row", "col", None, None), check_vma=False
    )
```

```python
import jax
import jax.numpy as jnp
from jax import lax
from jax.experimental import pallas as pl
from jax.experimental.pallas import tpu as pltpu
from jax.sharding import PartitionSpec as P


def assemble(blocks, block_offsets, block_live):
    slot_ids = jnp.arange(blocks.shape[1], dtype=jnp.int32)
    alive = slot_ids[None, :] < block_live[:, None]
    pieces = []
    for target in (-1, 0, 1):
        choose = (block_offsets == target) & alive
        total = jnp.zeros(blocks.shape[:1] + blocks.shape[2:], jnp.float32)
        for m in range(blocks.shape[1]):
            total = total + jnp.where(choose[:, m, None, None], blocks[:, m].astype(jnp.float32), 0.0)
        pieces.append(total.astype(jnp.bfloat16))
    return jnp.stack(pieces, axis=1)


def band_kernel(tile_rows, band_local, half_band, grid_tiles, sent_rows, row_count, col_count):
    extended = band_local + 2
    window = tile_rows + band_local - 1

    def kernel(ids, q_ref, jac_ref, recv_ref, mid_ref, left_ref, right_ref, up_ref, down_ref,
               up_right_ref, down_left_ref, out_ref, win_ref):
        row_id = ids[0]
        col_id = ids[1]
        first_row = row_id * tile_rows
        low_slot = col_id * band_local - 2
        low_offset = col_id * band_local - half_band
        size = jac_ref.shape[-1]

        for col_value in range(col_count):
            offset = col_value * band_local - half_band

            @pl.when(col_id == col_value)
            def _():
                for position in range(window):
                    at = offset + position
                    for g in range(3):
                        if at < 0:
                            win_ref[position, g] = recv_ref[sent_rows + at, g]
                        elif at < tile_rows:
                            win_ref[position, g] = jac_ref[at, g]
                        else:
                            win_ref[position, g] = recv_ref[at - tile_rows, g]

        def prior_tile(ext_row, ext_slot, masked):
            if ext_slot < 2:
                if ext_row == tile_rows + 1:
                    tile = down_left_ref[band_local - 2 + ext_slot]
                else:
                    tile = left_ref[ext_row - 1, band_local - 2 + ext_slot]
            elif ext_slot >= 2 + band_local:
                if ext_row == 0:
                    tile = up_right_ref[ext_slot - 2 - band_local]
                else:
                    tile = right_ref[ext_row - 1, ext_slot - 2 - band_local]
            elif ext_row == 0:
                tile = up_ref[ext_slot - 2]
            elif ext_row == tile_rows + 1:
                tile = down_ref[ext_slot - 2]
            else:
                tile = mid_ref[ext_row - 1, ext_slot - 2]
            if not masked:
                return tile
            column = first_row + ext_row - 1 + low_slot + ext_slot - half_band
            keep = (column >= 0) & (column < grid_tiles)
            return jnp.where(keep, tile, jnp.zeros_like(tile))

        eye = lax.broadcasted_iota(jnp.int32, (size, size), 0) == lax.broadcasted_iota(
            jnp.int32, (size, size), 1
        )

        def body(masked):
            for row in range(tile_rows):
                lhs = jnp.concatenate([jac_ref[row, f] for f in range(3)], axis=1)
                rhs = jnp.concatenate(
                    [
                        jnp.concatenate(
                            [prior_tile(row + f, u - f + 2, masked) for u in range(extended)], axis=1
                        )
                        for f in range(3)
                    ],
                    axis=0,
                )
                spread = jnp.dot(lhs, rhs, preferred_element_type=jnp.float32).astype(jnp.bfloat16)
                noise = jnp.where(eye, q_ref[pl.ds(row, 1), :], 0.0)
                for k in range(band_local):
                    left_side = spread[:, k * size : (k + 3) * size]
                    right_side = jnp.concatenate([win_ref[row + k, g] for g in range(3)], axis=1)
                    total = lax.dot_general(
                        left_side,
                        right_side,
                        (((1,), (1,)), ((), ())),
                        preferred_element_type=jnp.float32,
                    )
                    on_diagonal = (low_offset + k == 0).astype(jnp.float32)
                    total = total + noise * on_diagonal
                    if masked:
                        column = first_row + row + low_offset + k
                        keep = (column >= 0) & (column < grid_tiles)
                        total = jnp.where(keep, total, jnp.zeros_like(total))
                    out_ref[row, k] = total.astype(out_ref.dtype)

        edge = (row_id == 0) | (row_id == row_count - 1)

        @pl.when(edge)
        def _():
            body(True)

        @pl.when(jnp.logical_not(edge))
        def _():
            body(False)

    return kernel


def shards(p_band, blocks, block_offsets, block_live, q_var):
    tile_rows, band_local, tile_size = p_band.shape[0], p_band.shape[1], p_band.shape[2]
    row_count = lax.axis_size("row")
    col_count = lax.axis_size("col")
    half_band = band_local * col_count // 2
    grid_tiles = tile_rows * row_count
    row_id = lax.axis_index("row")
    col_id = lax.axis_index("col")
    low_offset = col_id * band_local - half_band

    def flat(a, b):
        return a * col_count + b

    left = lax.ppermute(p_band, "col", [(b, b + 1) for b in range(col_count - 1)])
    right = lax.ppermute(p_band, "col", [(b + 1, b) for b in range(col_count - 1)])
    up = lax.ppermute(p_band[-1], "row", [(a, a + 1) for a in range(row_count - 1)])
    down = lax.ppermute(p_band[0], "row", [(a + 1, a) for a in range(row_count - 1)])

    jacobian = assemble(blocks, block_offsets, block_live)

    sent_rows = half_band
    lower_half = col_id < col_count // 2
    send_start = jnp.where(lower_half, tile_rows - sent_rows, 0)
    sent = lax.dynamic_slice_in_dim(jacobian, send_start, sent_rows, 0)
    pairs = []
    for b in range(col_count):
        if b * band_local - half_band < 0:
            pairs += [(flat(a, b), flat(a + 1, b)) for a in range(row_count - 1)]
        else:
            pairs += [(flat(a, b), flat(a - 1, b)) for a in range(1, row_count)]
    received = lax.ppermute(sent, ("row", "col"), pairs)

    down_left = lax.ppermute(down, "col", [(b, b + 1) for b in range(col_count - 1)])
    up_right = lax.ppermute(up, "col", [(b + 1, b) for b in range(col_count - 1)])

    ids = jnp.stack([row_id, col_id]).astype(jnp.int32)
    vmem = pl.BlockSpec(memory_space=pltpu.MemorySpace.VMEM)
    smem = pl.BlockSpec(memory_space=pltpu.MemorySpace.SMEM)
    return pl.pallas_call(
        band_kernel(tile_rows, band_local, half_band, grid_tiles, sent_rows, row_count, col_count),
        out_shape=jax.ShapeDtypeStruct(p_band.shape, p_band.dtype),
        in_specs=[smem] + [vmem] * 10,
        out_specs=vmem,
        scratch_shapes=[pltpu.VMEM((tile_rows + band_local - 1, 3, tile_size, tile_size), p_band.dtype)],
    )(ids, q_var, jacobian, received, p_band, left, right, up, down, up_right, down_left)


def solution(mesh):
    placed = (
        P("row", "col", None, None),
        P("row", None, None, None),
        P("row", None),
        P("row"),
        P("row", None),
    )
    return jax.shard_map(
        shards, mesh=mesh, in_specs=placed, out_specs=P("row", "col", None, None), check_vma=False
    )
```

```python
import jax
import jax.numpy as jnp
from jax import lax
from jax.experimental import pallas as pl
from jax.experimental.pallas import tpu as pltpu
from jax.sharding import PartitionSpec as P


def assemble(blocks, block_offsets, block_live):
    slot_ids = jnp.arange(blocks.shape[1], dtype=jnp.int32)
    alive = slot_ids[None, :] < block_live[:, None]
    pieces = []
    for target in (-1, 0, 1):
        choose = (block_offsets == target) & alive
        total = jnp.zeros(blocks.shape[:1] + blocks.shape[2:], jnp.float32)
        for m in range(blocks.shape[1]):
            total = total + jnp.where(choose[:, m, None, None], blocks[:, m].astype(jnp.float32), 0.0)
        pieces.append(total.astype(jnp.bfloat16))
    return jnp.stack(pieces, axis=1)


def band_kernel(tile_rows, band_local, half_band, grid_tiles, sent_rows, row_count, col_count):
    extended = band_local + 2
    window = tile_rows + band_local - 1

    def kernel(ids, q_ref, jac_ref, recv_ref, mid_ref, left_ref, right_ref, up_ref, down_ref,
               up_right_ref, down_left_ref, out_ref, win_ref):
        row_id = ids[0]
        col_id = ids[1]
        first_row = row_id * tile_rows
        low_slot = col_id * band_local - 2
        low_offset = col_id * band_local - half_band
        size = jac_ref.shape[-1]

        for col_value in range(col_count):
            offset = col_value * band_local - half_band

            @pl.when(col_id == col_value)
            def _():
                for position in range(window):
                    at = offset + position
                    for g in range(3):
                        if at < 0:
                            win_ref[position, g] = recv_ref[sent_rows + at, g]
                        elif at < tile_rows:
                            win_ref[position, g] = jac_ref[at, g]
                        else:
                            win_ref[position, g] = recv_ref[at - tile_rows, g]

        def prior_tile(ext_row, ext_slot, masked):
            if ext_slot < 2:
                if ext_row == tile_rows + 1:
                    tile = down_left_ref[band_local - 2 + ext_slot]
                else:
                    tile = left_ref[ext_row - 1, band_local - 2 + ext_slot]
            elif ext_slot >= 2 + band_local:
                if ext_row == 0:
                    tile = up_right_ref[ext_slot - 2 - band_local]
                else:
                    tile = right_ref[ext_row - 1, ext_slot - 2 - band_local]
            elif ext_row == 0:
                tile = up_ref[ext_slot - 2]
            elif ext_row == tile_rows + 1:
                tile = down_ref[ext_slot - 2]
            else:
                tile = mid_ref[ext_row - 1, ext_slot - 2]
            if not masked:
                return tile
            column = first_row + ext_row - 1 + low_slot + ext_slot - half_band
            keep = (column >= 0) & (column < grid_tiles)
            return jnp.where(keep, tile, jnp.zeros_like(tile))

        eye = lax.broadcasted_iota(jnp.int32, (size, size), 0) == lax.broadcasted_iota(
            jnp.int32, (size, size), 1
        )

        def body(masked):
            for row in range(tile_rows):
                lhs = jnp.concatenate([jac_ref[row, f] for f in range(3)], axis=1)
                rhs = jnp.concatenate(
                    [
                        jnp.concatenate(
                            [prior_tile(row + f, u - f + 2, masked) for u in range(extended)], axis=1
                        )
                        for f in range(3)
                    ],
                    axis=0,
                )
                spread = jnp.dot(lhs, rhs, preferred_element_type=jnp.float32).astype(jnp.bfloat16)
                noise = jnp.where(eye, q_ref[pl.ds(row, 1), :], 0.0)
                for k in range(band_local):
                    left_side = spread[:, k * size : (k + 3) * size]
                    right_side = jnp.concatenate([win_ref[row + k, g] for g in range(3)], axis=1)
                    total = lax.dot_general(
                        left_side,
                        right_side,
                        (((1,), (1,)), ((), ())),
                        preferred_element_type=jnp.float32,
                    )
                    on_diagonal = (low_offset + k == 0).astype(jnp.float32)
                    total = total + noise * on_diagonal
                    if masked:
                        column = first_row + row + low_offset + k
                        keep = (column >= 0) & (column < grid_tiles)
                        total = jnp.where(keep, total, jnp.zeros_like(total))
                    out_ref[row, k] = total.astype(out_ref.dtype)

        edge = (row_id == 0) | (row_id == row_count - 1)

        @pl.when(edge)
        def _():
            body(True)

        @pl.when(jnp.logical_not(edge))
        def _():
            body(False)

    return kernel


def shards(p_band, blocks, block_offsets, block_live, q_var):
    tile_rows, band_local, tile_size = p_band.shape[0], p_band.shape[1], p_band.shape[2]
    row_count = lax.axis_size("row")
    col_count = lax.axis_size("col")
    half_band = band_local * col_count // 2
    grid_tiles = tile_rows * row_count
    row_id = lax.axis_index("row")
    col_id = lax.axis_index("col")
    low_offset = col_id * band_local - half_band

    def flat(a, b):
        return a * col_count + b

    left = lax.ppermute(p_band, "col", [(b, b + 1) for b in range(col_count - 1)])
    right = lax.ppermute(p_band, "col", [(b + 1, b) for b in range(col_count - 1)])
    meta = jnp.zeros((tile_size, tile_size), p_band.dtype)
    meta = meta.at[0, : tile_rows * 3].set(block_offsets.reshape(-1).astype(p_band.dtype))
    meta = meta.at[1, :tile_rows].set(block_live.astype(p_band.dtype))
    up_all = lax.ppermute(
        jnp.concatenate([p_band[-1], meta[None]], axis=0), "row", [(a, a + 1) for a in range(row_count - 1)]
    )
    down_all = lax.ppermute(
        jnp.concatenate([p_band[0], meta[None]], axis=0), "row", [(a + 1, a) for a in range(row_count - 1)]
    )
    up = up_all[:band_local]
    down = down_all[:band_local]

    sent_rows = half_band
    lower_half = col_id < col_count // 2
    send_start = jnp.where(lower_half, tile_rows - sent_rows, 0)
    sent = lax.dynamic_slice_in_dim(blocks, send_start, sent_rows, 0)
    pairs = []
    for b in range(col_count):
        if b * band_local - half_band < 0:
            pairs += [(flat(a, b), flat(a + 1, b)) for a in range(row_count - 1)]
        else:
            pairs += [(flat(a, b), flat(a - 1, b)) for a in range(1, row_count)]
    received_blocks = lax.ppermute(sent, ("row", "col"), pairs)

    jacobian = assemble(blocks, block_offsets, block_live)
    received_meta = jnp.where(lower_half, up_all[band_local], down_all[band_local]).astype(jnp.float32)
    received_offsets = jnp.round(received_meta[0, : tile_rows * 3]).astype(jnp.int32).reshape(tile_rows, 3)
    received_live = jnp.round(received_meta[1, :tile_rows]).astype(jnp.int32)
    received = assemble(
        received_blocks,
        lax.dynamic_slice_in_dim(received_offsets, send_start, sent_rows, 0),
        lax.dynamic_slice_in_dim(received_live, send_start, sent_rows, 0),
    )

    down_left = lax.ppermute(down, "col", [(b, b + 1) for b in range(col_count - 1)])
    up_right = lax.ppermute(up, "col", [(b + 1, b) for b in range(col_count - 1)])

    ids = jnp.stack([row_id, col_id]).astype(jnp.int32)
    vmem = pl.BlockSpec(memory_space=pltpu.MemorySpace.VMEM)
    smem = pl.BlockSpec(memory_space=pltpu.MemorySpace.SMEM)
    return pl.pallas_call(
        band_kernel(tile_rows, band_local, half_band, grid_tiles, sent_rows, row_count, col_count),
        out_shape=jax.ShapeDtypeStruct(p_band.shape, p_band.dtype),
        in_specs=[smem] + [vmem] * 10,
        out_specs=vmem,
        scratch_shapes=[pltpu.VMEM((tile_rows + band_local - 1, 3, tile_size, tile_size), p_band.dtype)],
    )(ids, q_var, jacobian, received, p_band, left, right, up, down, up_right, down_left)


def solution(mesh):
    placed = (
        P("row", "col", None, None),
        P("row", None, None, None),
        P("row", None),
        P("row"),
        P("row", None),
    )
    return jax.shard_map(
        shards, mesh=mesh, in_specs=placed, out_specs=P("row", "col", None, None), check_vma=False
    )
```

```python
import jax
import jax.numpy as jnp
from jax import lax
from jax.experimental import pallas as pl
from jax.experimental.pallas import tpu as pltpu
from jax.sharding import PartitionSpec as P


def assemble(blocks, block_offsets, block_live):
    slot_ids = jnp.arange(blocks.shape[1], dtype=jnp.int32)
    alive = slot_ids[None, :] < block_live[:, None]
    pieces = []
    for target in (-1, 0, 1):
        choose = (block_offsets == target) & alive
        total = jnp.zeros(blocks.shape[:1] + blocks.shape[2:], jnp.float32)
        for m in range(blocks.shape[1]):
            total = total + jnp.where(choose[:, m, None, None], blocks[:, m].astype(jnp.float32), 0.0)
        pieces.append(total.astype(jnp.bfloat16))
    return jnp.stack(pieces, axis=1)


def band_kernel(tile_rows, band_local, half_band, grid_tiles, sent_rows, row_count, col_count):
    extended = band_local + 2
    window = tile_rows + band_local - 1

    def kernel(ids, q_ref, jac_ref, recv_ref, mid_ref, left_ref, right_ref, up_ref, down_ref,
               up_right_ref, down_left_ref, out_ref, win_ref):
        row_id = ids[0]
        col_id = ids[1]
        first_row = row_id * tile_rows
        low_slot = col_id * band_local - 2
        low_offset = col_id * band_local - half_band
        size = jac_ref.shape[-1]

        for col_value in range(col_count):
            offset = col_value * band_local - half_band

            @pl.when(col_id == col_value)
            def _():
                for position in range(window):
                    at = offset + position
                    for g in range(3):
                        if at < 0:
                            win_ref[position, g] = recv_ref[sent_rows + at, g]
                        elif at < tile_rows:
                            win_ref[position, g] = jac_ref[at, g]
                        else:
                            win_ref[position, g] = recv_ref[at - tile_rows, g]

        def prior_tile(ext_row, ext_slot, masked):
            if ext_slot < 2:
                if ext_row == tile_rows + 1:
                    tile = down_left_ref[band_local - 2 + ext_slot]
                else:
                    tile = left_ref[ext_row - 1, band_local - 2 + ext_slot]
            elif ext_slot >= 2 + band_local:
                if ext_row == 0:
                    tile = up_right_ref[ext_slot - 2 - band_local]
                else:
                    tile = right_ref[ext_row - 1, ext_slot - 2 - band_local]
            elif ext_row == 0:
                tile = up_ref[ext_slot - 2]
            elif ext_row == tile_rows + 1:
                tile = down_ref[ext_slot - 2]
            else:
                tile = mid_ref[ext_row - 1, ext_slot - 2]
            if not masked:
                return tile
            column = first_row + ext_row - 1 + low_slot + ext_slot - half_band
            keep = (column >= 0) & (column < grid_tiles)
            return jnp.where(keep, tile, jnp.zeros_like(tile))

        eye = lax.broadcasted_iota(jnp.int32, (size, size), 0) == lax.broadcasted_iota(
            jnp.int32, (size, size), 1
        )

        def body(masked):
            for row in range(tile_rows):
                lhs = jnp.concatenate([jac_ref[row, f] for f in range(3)], axis=1)
                rhs = jnp.concatenate(
                    [
                        jnp.concatenate(
                            [prior_tile(row + f, u - f + 2, masked) for u in range(extended)], axis=1
                        )
                        for f in range(3)
                    ],
                    axis=0,
                )
                spread = jnp.dot(lhs, rhs, preferred_element_type=jnp.float32).astype(jnp.bfloat16)
                noise = jnp.where(eye, q_ref[pl.ds(row, 1), :], 0.0)
                for k in range(band_local):
                    left_side = spread[:, k * size : (k + 3) * size]
                    right_side = jnp.concatenate([win_ref[row + k, g] for g in range(3)], axis=1)
                    total = lax.dot_general(
                        left_side,
                        right_side,
                        (((1,), (1,)), ((), ())),
                        preferred_element_type=jnp.float32,
                    )
                    on_diagonal = (low_offset + k == 0).astype(jnp.float32)
                    total = total + noise * on_diagonal
                    if masked:
                        column = first_row + row + low_offset + k
                        keep = (column >= 0) & (column < grid_tiles)
                        total = jnp.where(keep, total, jnp.zeros_like(total))
                    out_ref[row, k] = total.astype(out_ref.dtype)

        edge = (row_id == 0) | (row_id == row_count - 1)

        @pl.when(edge)
        def _():
            body(True)

        @pl.when(jnp.logical_not(edge))
        def _():
            body(False)

    return kernel


def shards(p_band, blocks, block_offsets, block_live, q_var):
    tile_rows, band_local, tile_size = p_band.shape[0], p_band.shape[1], p_band.shape[2]
    row_count = lax.axis_size("row")
    col_count = lax.axis_size("col")
    half_band = band_local * col_count // 2
    grid_tiles = tile_rows * row_count
    row_id = lax.axis_index("row")
    col_id = lax.axis_index("col")
    low_offset = col_id * band_local - half_band

    def flat(a, b):
        return a * col_count + b

    left = lax.ppermute(p_band, "col", [(b, b + 1) for b in range(col_count - 1)])
    right = lax.ppermute(p_band, "col", [(b + 1, b) for b in range(col_count - 1)])
    meta = jnp.zeros((tile_size, tile_size), p_band.dtype)
    meta = meta.at[0, : tile_rows * 3].set(block_offsets.reshape(-1).astype(p_band.dtype))
    meta = meta.at[1, :tile_rows].set(block_live.astype(p_band.dtype))
    up_all = lax.ppermute(
        jnp.concatenate([p_band[-1], meta[None]], axis=0), "row", [(a, a + 1) for a in range(row_count - 1)]
    )
    down_all = lax.ppermute(
        jnp.concatenate([p_band[0], meta[None]], axis=0), "row", [(a + 1, a) for a in range(row_count - 1)]
    )
    up = up_all[:band_local]
    down = down_all[:band_local]

    sent_rows = half_band
    lower_half = col_id < col_count // 2
    send_start = jnp.where(lower_half, tile_rows - sent_rows, 0)
    sent = lax.dynamic_slice_in_dim(blocks, send_start, sent_rows, 0)
    pairs = []
    for b in range(col_count):
        if b * band_local - half_band < 0:
            pairs += [(flat(a, b), flat(a + 1, b)) for a in range(row_count - 1)]
        else:
            pairs += [(flat(a, b), flat(a - 1, b)) for a in range(1, row_count)]
    sent, _ = lax.optimization_barrier((sent, (up_all, down_all)))
    received_blocks = lax.ppermute(sent, ("row", "col"), pairs)

    jacobian = assemble(blocks, block_offsets, block_live)
    received_meta = jnp.where(lower_half, up_all[band_local], down_all[band_local]).astype(jnp.float32)
    received_offsets = jnp.round(received_meta[0, : tile_rows * 3]).astype(jnp.int32).reshape(tile_rows, 3)
    received_live = jnp.round(received_meta[1, :tile_rows]).astype(jnp.int32)
    received = assemble(
        received_blocks,
        lax.dynamic_slice_in_dim(received_offsets, send_start, sent_rows, 0),
        lax.dynamic_slice_in_dim(received_live, send_start, sent_rows, 0),
    )

    down_left = lax.ppermute(down, "col", [(b, b + 1) for b in range(col_count - 1)])
    up_right = lax.ppermute(up, "col", [(b + 1, b) for b in range(col_count - 1)])

    ids = jnp.stack([row_id, col_id]).astype(jnp.int32)
    vmem = pl.BlockSpec(memory_space=pltpu.MemorySpace.VMEM)
    smem = pl.BlockSpec(memory_space=pltpu.MemorySpace.SMEM)
    return pl.pallas_call(
        band_kernel(tile_rows, band_local, half_band, grid_tiles, sent_rows, row_count, col_count),
        out_shape=jax.ShapeDtypeStruct(p_band.shape, p_band.dtype),
        in_specs=[smem] + [vmem] * 10,
        out_specs=vmem,
        scratch_shapes=[pltpu.VMEM((tile_rows + band_local - 1, 3, tile_size, tile_size), p_band.dtype)],
    )(ids, q_var, jacobian, received, p_band, left, right, up, down, up_right, down_left)


def solution(mesh):
    placed = (
        P("row", "col", None, None),
        P("row", None, None, None),
        P("row", None),
        P("row"),
        P("row", None),
    )
    return jax.shard_map(
        shards, mesh=mesh, in_specs=placed, out_specs=P("row", "col", None, None), check_vma=False
    )
```

```python
import jax
import jax.numpy as jnp
from jax import lax
from jax.experimental import pallas as pl
from jax.experimental.pallas import tpu as pltpu
from jax.sharding import PartitionSpec as P


def assemble(blocks, block_offsets, block_live):
    slot_ids = jnp.arange(blocks.shape[1], dtype=jnp.int32)
    alive = slot_ids[None, :] < block_live[:, None]
    pieces = []
    for target in (-1, 0, 1):
        choose = (block_offsets == target) & alive
        total = jnp.zeros(blocks.shape[:1] + blocks.shape[2:], jnp.float32)
        for m in range(blocks.shape[1]):
            total = total + jnp.where(choose[:, m, None, None], blocks[:, m].astype(jnp.float32), 0.0)
        pieces.append(total.astype(jnp.bfloat16))
    return jnp.stack(pieces, axis=1)


def band_kernel(tile_rows, band_local, half_band, grid_tiles, sent_rows, row_count, col_count):
    extended = band_local + 2
    window = tile_rows + band_local - 1

    def kernel(ids, q_ref, jac_ref, recv_ref, mid_ref, left_ref, right_ref, up_ref, down_ref,
               out_ref, win_ref):
        row_id = ids[0]
        col_id = ids[1]
        first_row = row_id * tile_rows
        low_slot = col_id * band_local - 2
        low_offset = col_id * band_local - half_band
        size = jac_ref.shape[-1]

        for col_value in range(col_count):
            offset = col_value * band_local - half_band

            @pl.when(col_id == col_value)
            def _():
                for position in range(window):
                    at = offset + position
                    for g in range(3):
                        if at < 0:
                            win_ref[position, g] = recv_ref[sent_rows + at, g]
                        elif at < tile_rows:
                            win_ref[position, g] = jac_ref[at, g]
                        else:
                            win_ref[position, g] = recv_ref[at - tile_rows, g]

        def prior_tile(ext_row, ext_slot, masked):
            if ext_slot < 2:
                tile = left_ref[ext_row - 1, band_local - 2 + ext_slot]
            elif ext_slot >= 2 + band_local:
                tile = right_ref[ext_row, ext_slot - 2 - band_local]
            elif ext_row == 0:
                tile = up_ref[ext_slot - 2]
            elif ext_row == tile_rows + 1:
                tile = down_ref[ext_slot - 2]
            else:
                tile = mid_ref[ext_row - 1, ext_slot - 2]
            if not masked:
                return tile
            column = first_row + ext_row - 1 + low_slot + ext_slot - half_band
            keep = (column >= 0) & (column < grid_tiles)
            return jnp.where(keep, tile, jnp.zeros_like(tile))

        eye = lax.broadcasted_iota(jnp.int32, (size, size), 0) == lax.broadcasted_iota(
            jnp.int32, (size, size), 1
        )

        def body(masked):
            for row in range(tile_rows):
                lhs = jnp.concatenate([jac_ref[row, f] for f in range(3)], axis=1)
                rhs = jnp.concatenate(
                    [
                        jnp.concatenate(
                            [prior_tile(row + f, u - f + 2, masked) for u in range(extended)], axis=1
                        )
                        for f in range(3)
                    ],
                    axis=0,
                )
                spread = jnp.dot(lhs, rhs, preferred_element_type=jnp.float32).astype(jnp.bfloat16)
                noise = jnp.where(eye, q_ref[pl.ds(row, 1), :], 0.0)
                for k in range(band_local):
                    left_side = spread[:, k * size : (k + 3) * size]
                    right_side = jnp.concatenate([win_ref[row + k, g] for g in range(3)], axis=1)
                    total = lax.dot_general(
                        left_side,
                        right_side,
                        (((1,), (1,)), ((), ())),
                        preferred_element_type=jnp.float32,
                    )
                    on_diagonal = (low_offset + k == 0).astype(jnp.float32)
                    total = total + noise * on_diagonal
                    if masked:
                        column = first_row + row + low_offset + k
                        keep = (column >= 0) & (column < grid_tiles)
                        total = jnp.where(keep, total, jnp.zeros_like(total))
                    out_ref[row, k] = total.astype(out_ref.dtype)

        edge = (row_id == 0) | (row_id == row_count - 1)

        @pl.when(edge)
        def _():
            body(True)

        @pl.when(jnp.logical_not(edge))
        def _():
            body(False)

    return kernel


def shards(p_band, blocks, block_offsets, block_live, q_var):
    tile_rows, band_local, tile_size = p_band.shape[0], p_band.shape[1], p_band.shape[2]
    row_count = lax.axis_size("row")
    col_count = lax.axis_size("col")
    half_band = band_local * col_count // 2
    grid_tiles = tile_rows * row_count
    row_id = lax.axis_index("row")
    col_id = lax.axis_index("col")
    low_offset = col_id * band_local - half_band

    def flat(a, b):
        return a * col_count + b

    meta = jnp.zeros((tile_size, tile_size), p_band.dtype)
    meta = meta.at[0, : tile_rows * 3].set(block_offsets.reshape(-1).astype(p_band.dtype))
    meta = meta.at[1, :tile_rows].set(block_live.astype(p_band.dtype))
    up_all = lax.ppermute(
        jnp.concatenate([p_band[-1], meta[None]], axis=0), "row", [(a, a + 1) for a in range(row_count - 1)]
    )
    down_all = lax.ppermute(
        jnp.concatenate([p_band[0], meta[None]], axis=0), "row", [(a + 1, a) for a in range(row_count - 1)]
    )
    up = up_all[:band_local]
    down = down_all[:band_local]

    sent_rows = half_band
    lower_half = col_id < col_count // 2
    send_start = jnp.where(lower_half, tile_rows - sent_rows, 0)
    sent = lax.dynamic_slice_in_dim(blocks, send_start, sent_rows, 0)
    pairs = []
    for b in range(col_count):
        if b * band_local - half_band < 0:
            pairs += [(flat(a, b), flat(a + 1, b)) for a in range(row_count - 1)]
        else:
            pairs += [(flat(a, b), flat(a - 1, b)) for a in range(1, row_count)]
    left_payload = jnp.concatenate([p_band, down[None]], axis=0)
    right_payload = jnp.concatenate([up[None], p_band], axis=0)
    left = lax.ppermute(left_payload, "col", [(b, b + 1) for b in range(col_count - 1)])
    right = lax.ppermute(right_payload, "col", [(b + 1, b) for b in range(col_count - 1)])
    sent, _ = lax.optimization_barrier((sent, (up_all, down_all)))
    received_blocks = lax.ppermute(sent, ("row", "col"), pairs)

    jacobian = assemble(blocks, block_offsets, block_live)
    received_meta = jnp.where(lower_half, up_all[band_local], down_all[band_local]).astype(jnp.float32)
    received_offsets = jnp.round(received_meta[0, : tile_rows * 3]).astype(jnp.int32).reshape(tile_rows, 3)
    received_live = jnp.round(received_meta[1, :tile_rows]).astype(jnp.int32)
    received = assemble(
        received_blocks,
        lax.dynamic_slice_in_dim(received_offsets, send_start, sent_rows, 0),
        lax.dynamic_slice_in_dim(received_live, send_start, sent_rows, 0),
    )

    ids = jnp.stack([row_id, col_id]).astype(jnp.int32)
    vmem = pl.BlockSpec(memory_space=pltpu.MemorySpace.VMEM)
    smem = pl.BlockSpec(memory_space=pltpu.MemorySpace.SMEM)
    return pl.pallas_call(
        band_kernel(tile_rows, band_local, half_band, grid_tiles, sent_rows, row_count, col_count),
        out_shape=jax.ShapeDtypeStruct(p_band.shape, p_band.dtype),
        in_specs=[smem] + [vmem] * 8,
        out_specs=vmem,
        scratch_shapes=[pltpu.VMEM((tile_rows + band_local - 1, 3, tile_size, tile_size), p_band.dtype)],
    )(ids, q_var, jacobian, received, p_band, left, right, up, down)


def solution(mesh):
    placed = (
        P("row", "col", None, None),
        P("row", None, None, None),
        P("row", None),
        P("row"),
        P("row", None),
    )
    return jax.shard_map(
        shards, mesh=mesh, in_specs=placed, out_specs=P("row", "col", None, None), check_vma=False
    )
```

```python
import jax
import jax.numpy as jnp
from jax import lax
from jax.experimental import pallas as pl
from jax.experimental.pallas import tpu as pltpu
from jax.sharding import PartitionSpec as P


def assemble(blocks, block_offsets, block_live):
    slot_ids = jnp.arange(blocks.shape[1], dtype=jnp.int32)
    alive = slot_ids[None, :] < block_live[:, None]
    pieces = []
    for target in (-1, 0, 1):
        choose = (block_offsets == target) & alive
        total = jnp.zeros(blocks.shape[:1] + blocks.shape[2:], jnp.float32)
        for m in range(blocks.shape[1]):
            total = total + jnp.where(choose[:, m, None, None], blocks[:, m].astype(jnp.float32), 0.0)
        pieces.append(total.astype(jnp.bfloat16))
    return jnp.stack(pieces, axis=1)


def band_kernel(tile_rows, band_local, half_band, grid_tiles, sent_rows, row_count, col_count):
    extended = band_local + 2
    window = tile_rows + band_local - 1

    def kernel(ids, q_ref, jac_ref, recv_ref, mid_ref, left_ref, right_ref, up_ref, down_ref,
               up_right_ref, down_left_ref, out_ref, win_ref):
        row_id = ids[0]
        col_id = ids[1]
        first_row = row_id * tile_rows
        low_slot = col_id * band_local - 2
        low_offset = col_id * band_local - half_band
        size = jac_ref.shape[-1]

        for col_value in range(col_count):
            offset = col_value * band_local - half_band

            @pl.when(col_id == col_value)
            def _():
                for position in range(window):
                    at = offset + position
                    for g in range(3):
                        if at < 0:
                            win_ref[position, g] = recv_ref[sent_rows + at, g]
                        elif at < tile_rows:
                            win_ref[position, g] = jac_ref[at, g]
                        else:
                            win_ref[position, g] = recv_ref[at - tile_rows, g]

        def prior_tile(ext_row, ext_slot, masked):
            if ext_slot < 2:
                if ext_row == tile_rows + 1:
                    tile = down_left_ref[band_local - 2 + ext_slot]
                else:
                    tile = left_ref[ext_row - 1, band_local - 2 + ext_slot]
            elif ext_slot >= 2 + band_local:
                if ext_row == 0:
                    tile = up_right_ref[ext_slot - 2 - band_local]
                else:
                    tile = right_ref[ext_row - 1, ext_slot - 2 - band_local]
            elif ext_row == 0:
                tile = up_ref[ext_slot - 2]
            elif ext_row == tile_rows + 1:
                tile = down_ref[ext_slot - 2]
            else:
                tile = mid_ref[ext_row - 1, ext_slot - 2]
            if not masked:
                return tile
            column = first_row + ext_row - 1 + low_slot + ext_slot - half_band
            keep = (column >= 0) & (column < grid_tiles)
            return jnp.where(keep, tile, jnp.zeros_like(tile))

        eye = lax.broadcasted_iota(jnp.int32, (size, size), 0) == lax.broadcasted_iota(
            jnp.int32, (size, size), 1
        )

        def body(masked):
            for row in range(tile_rows):
                spread = []
                for u in range(extended):
                    acc = None
                    for f in range(3):
                        term = jnp.dot(
                            jac_ref[row, f],
                            prior_tile(row + f, u - f + 2, masked),
                            preferred_element_type=jnp.float32,
                        )
                        acc = term if acc is None else acc + term
                    spread.append(acc.astype(jnp.bfloat16))
                noise = jnp.where(eye, q_ref[pl.ds(row, 1), :], 0.0)
                for k in range(band_local):
                    total = None
                    for g in range(3):
                        term = lax.dot_general(
                            spread[k + g],
                            win_ref[row + k, g],
                            (((1,), (1,)), ((), ())),
                            preferred_element_type=jnp.float32,
                        )
                        total = term if total is None else total + term
                    on_diagonal = (low_offset + k == 0).astype(jnp.float32)
                    total = total + noise * on_diagonal
                    if masked:
                        column = first_row + row + low_offset + k
                        keep = (column >= 0) & (column < grid_tiles)
                        total = jnp.where(keep, total, jnp.zeros_like(total))
                    out_ref[row, k] = total.astype(out_ref.dtype)

        edge = (row_id == 0) | (row_id == row_count - 1)

        @pl.when(edge)
        def _():
            body(True)

        @pl.when(jnp.logical_not(edge))
        def _():
            body(False)

    return kernel


def shards(p_band, blocks, block_offsets, block_live, q_var):
    tile_rows, band_local, tile_size = p_band.shape[0], p_band.shape[1], p_band.shape[2]
    row_count = lax.axis_size("row")
    col_count = lax.axis_size("col")
    half_band = band_local * col_count // 2
    grid_tiles = tile_rows * row_count
    row_id = lax.axis_index("row")
    col_id = lax.axis_index("col")
    low_offset = col_id * band_local - half_band

    def flat(a, b):
        return a * col_count + b

    left = lax.ppermute(p_band, "col", [(b, b + 1) for b in range(col_count - 1)])
    right = lax.ppermute(p_band, "col", [(b + 1, b) for b in range(col_count - 1)])
    meta = jnp.zeros((tile_size, tile_size), p_band.dtype)
    meta = meta.at[0, : tile_rows * 3].set(block_offsets.reshape(-1).astype(p_band.dtype))
    meta = meta.at[1, :tile_rows].set(block_live.astype(p_band.dtype))
    up_all = lax.ppermute(
        jnp.concatenate([p_band[-1], meta[None]], axis=0), "row", [(a, a + 1) for a in range(row_count - 1)]
    )
    down_all = lax.ppermute(
        jnp.concatenate([p_band[0], meta[None]], axis=0), "row", [(a + 1, a) for a in range(row_count - 1)]
    )
    up = up_all[:band_local]
    down = down_all[:band_local]

    sent_rows = half_band
    lower_half = col_id < col_count // 2
    send_start = jnp.where(lower_half, tile_rows - sent_rows, 0)
    sent = lax.dynamic_slice_in_dim(blocks, send_start, sent_rows, 0)
    pairs = []
    for b in range(col_count):
        if b * band_local - half_band < 0:
            pairs += [(flat(a, b), flat(a + 1, b)) for a in range(row_count - 1)]
        else:
            pairs += [(flat(a, b), flat(a - 1, b)) for a in range(1, row_count)]
    received_blocks = lax.ppermute(sent, ("row", "col"), pairs)

    jacobian = assemble(blocks, block_offsets, block_live)
    received_meta = jnp.where(lower_half, up_all[band_local], down_all[band_local]).astype(jnp.float32)
    received_offsets = jnp.round(received_meta[0, : tile_rows * 3]).astype(jnp.int32).reshape(tile_rows, 3)
    received_live = jnp.round(received_meta[1, :tile_rows]).astype(jnp.int32)
    received = assemble(
        received_blocks,
        lax.dynamic_slice_in_dim(received_offsets, send_start, sent_rows, 0),
        lax.dynamic_slice_in_dim(received_live, send_start, sent_rows, 0),
    )

    down_left = lax.ppermute(down, "col", [(b, b + 1) for b in range(col_count - 1)])
    up_right = lax.ppermute(up, "col", [(b + 1, b) for b in range(col_count - 1)])

    ids = jnp.stack([row_id, col_id]).astype(jnp.int32)
    vmem = pl.BlockSpec(memory_space=pltpu.MemorySpace.VMEM)
    smem = pl.BlockSpec(memory_space=pltpu.MemorySpace.SMEM)
    return pl.pallas_call(
        band_kernel(tile_rows, band_local, half_band, grid_tiles, sent_rows, row_count, col_count),
        out_shape=jax.ShapeDtypeStruct(p_band.shape, p_band.dtype),
        in_specs=[smem] + [vmem] * 10,
        out_specs=vmem,
        scratch_shapes=[pltpu.VMEM((tile_rows + band_local - 1, 3, tile_size, tile_size), p_band.dtype)],
    )(ids, q_var, jacobian, received, p_band, left, right, up, down, up_right, down_left)


def solution(mesh):
    placed = (
        P("row", "col", None, None),
        P("row", None, None, None),
        P("row", None),
        P("row"),
        P("row", None),
    )
    return jax.shard_map(
        shards, mesh=mesh, in_specs=placed, out_specs=P("row", "col", None, None), check_vma=False
    )
```

```python
import jax
import jax.numpy as jnp
from jax import lax
from jax.experimental import pallas as pl
from jax.experimental.pallas import tpu as pltpu
from jax.sharding import PartitionSpec as P


def assemble(blocks, block_offsets, block_live):
    slot_ids = jnp.arange(blocks.shape[1], dtype=jnp.int32)
    alive = slot_ids[None, :] < block_live[:, None]
    pieces = []
    for target in (-1, 0, 1):
        choose = (block_offsets == target) & alive
        total = jnp.zeros(blocks.shape[:1] + blocks.shape[2:], jnp.float32)
        for m in range(blocks.shape[1]):
            total = total + jnp.where(choose[:, m, None, None], blocks[:, m].astype(jnp.float32), 0.0)
        pieces.append(total.astype(jnp.bfloat16))
    return jnp.stack(pieces, axis=1)


def band_kernel(tile_rows, band_local, half_band, grid_tiles, sent_rows, row_count, col_count):
    extended = band_local + 2
    window = tile_rows + band_local - 1

    def kernel(ids, q_ref, jac_ref, recv_ref, mid_ref, left_ref, right_ref, up_ref, down_ref,
               up_right_ref, down_left_ref, out_ref, win_ref, spread_ref):
        row_id = ids[0]
        col_id = ids[1]
        first_row = row_id * tile_rows
        low_slot = col_id * band_local - 2
        low_offset = col_id * band_local - half_band
        size = jac_ref.shape[-1]

        for col_value in range(col_count):
            offset = col_value * band_local - half_band

            @pl.when(col_id == col_value)
            def _():
                for position in range(window):
                    at = offset + position
                    for g in range(3):
                        if at < 0:
                            win_ref[position, g] = recv_ref[sent_rows + at, g]
                        elif at < tile_rows:
                            win_ref[position, g] = jac_ref[at, g]
                        else:
                            win_ref[position, g] = recv_ref[at - tile_rows, g]

        def prior_tile(ext_row, ext_slot, masked):
            if ext_slot < 2:
                if ext_row == tile_rows + 1:
                    tile = down_left_ref[band_local - 2 + ext_slot]
                else:
                    tile = left_ref[ext_row - 1, band_local - 2 + ext_slot]
            elif ext_slot >= 2 + band_local:
                if ext_row == 0:
                    tile = up_right_ref[ext_slot - 2 - band_local]
                else:
                    tile = right_ref[ext_row - 1, ext_slot - 2 - band_local]
            elif ext_row == 0:
                tile = up_ref[ext_slot - 2]
            elif ext_row == tile_rows + 1:
                tile = down_ref[ext_slot - 2]
            else:
                tile = mid_ref[ext_row - 1, ext_slot - 2]
            if not masked:
                return tile
            column = first_row + ext_row - 1 + low_slot + ext_slot - half_band
            keep = (column >= 0) & (column < grid_tiles)
            return jnp.where(keep, tile, jnp.zeros_like(tile))

        eye = lax.broadcasted_iota(jnp.int32, (size, size), 0) == lax.broadcasted_iota(
            jnp.int32, (size, size), 1
        )

        def body(masked):
            for row in range(tile_rows):
                lhs = jnp.concatenate([jac_ref[row, f] for f in range(3)], axis=1)
                rhs = jnp.concatenate(
                    [
                        jnp.concatenate(
                            [prior_tile(row + f, u - f + 2, masked) for u in range(extended)], axis=1
                        )
                        for f in range(3)
                    ],
                    axis=0,
                )
                spread_ref[row] = jnp.dot(lhs, rhs, preferred_element_type=jnp.float32).astype(
                    jnp.bfloat16
                )
            for position in range(window):
                members = [
                    (position - k, k) for k in range(band_local) if 0 <= position - k < tile_rows
                ]
                left_side = jnp.concatenate(
                    [spread_ref[row, :, k * size : (k + 3) * size] for row, k in members], axis=0
                )
                right_side = jnp.concatenate([win_ref[position, g] for g in range(3)], axis=1)
                product = lax.dot_general(
                    left_side,
                    right_side,
                    (((1,), (1,)), ((), ())),
                    preferred_element_type=jnp.float32,
                )
                for index, (row, k) in enumerate(members):
                    total = product[index * size : (index + 1) * size]
                    on_diagonal = (low_offset + k == 0).astype(jnp.float32)
                    noise = jnp.where(eye, q_ref[pl.ds(row, 1), :], 0.0)
                    total = total + noise * on_diagonal
                    if masked:
                        column = first_row + row + low_offset + k
                        keep = (column >= 0) & (column < grid_tiles)
                        total = jnp.where(keep, total, jnp.zeros_like(total))
                    out_ref[row, k] = total.astype(out_ref.dtype)

        edge = (row_id == 0) | (row_id == row_count - 1)

        @pl.when(edge)
        def _():
            body(True)

        @pl.when(jnp.logical_not(edge))
        def _():
            body(False)

    return kernel


def shards(p_band, blocks, block_offsets, block_live, q_var):
    tile_rows, band_local, tile_size = p_band.shape[0], p_band.shape[1], p_band.shape[2]
    row_count = lax.axis_size("row")
    col_count = lax.axis_size("col")
    half_band = band_local * col_count // 2
    grid_tiles = tile_rows * row_count
    row_id = lax.axis_index("row")
    col_id = lax.axis_index("col")
    low_offset = col_id * band_local - half_band

    def flat(a, b):
        return a * col_count + b

    left = lax.ppermute(p_band, "col", [(b, b + 1) for b in range(col_count - 1)])
    right = lax.ppermute(p_band, "col", [(b + 1, b) for b in range(col_count - 1)])
    meta = jnp.zeros((tile_size, tile_size), p_band.dtype)
    meta = meta.at[0, : tile_rows * 3].set(block_offsets.reshape(-1).astype(p_band.dtype))
    meta = meta.at[1, :tile_rows].set(block_live.astype(p_band.dtype))
    up_all = lax.ppermute(
        jnp.concatenate([p_band[-1], meta[None]], axis=0), "row", [(a, a + 1) for a in range(row_count - 1)]
    )
    down_all = lax.ppermute(
        jnp.concatenate([p_band[0], meta[None]], axis=0), "row", [(a + 1, a) for a in range(row_count - 1)]
    )
    up = up_all[:band_local]
    down = down_all[:band_local]

    sent_rows = half_band
    lower_half = col_id < col_count // 2
    send_start = jnp.where(lower_half, tile_rows - sent_rows, 0)
    sent = lax.dynamic_slice_in_dim(blocks, send_start, sent_rows, 0)
    pairs = []
    for b in range(col_count):
        if b * band_local - half_band < 0:
            pairs += [(flat(a, b), flat(a + 1, b)) for a in range(row_count - 1)]
        else:
            pairs += [(flat(a, b), flat(a - 1, b)) for a in range(1, row_count)]
    received_blocks = lax.ppermute(sent, ("row", "col"), pairs)

    jacobian = assemble(blocks, block_offsets, block_live)
    received_meta = jnp.where(lower_half, up_all[band_local], down_all[band_local]).astype(jnp.float32)
    received_offsets = jnp.round(received_meta[0, : tile_rows * 3]).astype(jnp.int32).reshape(tile_rows, 3)
    received_live = jnp.round(received_meta[1, :tile_rows]).astype(jnp.int32)
    received = assemble(
        received_blocks,
        lax.dynamic_slice_in_dim(received_offsets, send_start, sent_rows, 0),
        lax.dynamic_slice_in_dim(received_live, send_start, sent_rows, 0),
    )

    down_left = lax.ppermute(down, "col", [(b, b + 1) for b in range(col_count - 1)])
    up_right = lax.ppermute(up, "col", [(b + 1, b) for b in range(col_count - 1)])

    ids = jnp.stack([row_id, col_id]).astype(jnp.int32)
    vmem = pl.BlockSpec(memory_space=pltpu.MemorySpace.VMEM)
    smem = pl.BlockSpec(memory_space=pltpu.MemorySpace.SMEM)
    return pl.pallas_call(
        band_kernel(tile_rows, band_local, half_band, grid_tiles, sent_rows, row_count, col_count),
        out_shape=jax.ShapeDtypeStruct(p_band.shape, p_band.dtype),
        in_specs=[smem] + [vmem] * 10,
        out_specs=vmem,
        scratch_shapes=[
            pltpu.VMEM((tile_rows + band_local - 1, 3, tile_size, tile_size), p_band.dtype),
            pltpu.VMEM((tile_rows, tile_size, (band_local + 2) * tile_size), p_band.dtype),
        ],
    )(ids, q_var, jacobian, received, p_band, left, right, up, down, up_right, down_left)


def solution(mesh):
    placed = (
        P("row", "col", None, None),
        P("row", None, None, None),
        P("row", None),
        P("row"),
        P("row", None),
    )
    return jax.shard_map(
        shards, mesh=mesh, in_specs=placed, out_specs=P("row", "col", None, None), check_vma=False
    )
```

```python
import jax
import jax.numpy as jnp
from jax import lax
from jax.experimental import pallas as pl
from jax.experimental.pallas import tpu as pltpu
from jax.sharding import PartitionSpec as P


def assemble(blocks, block_offsets, block_live):
    slot_ids = jnp.arange(blocks.shape[1], dtype=jnp.int32)
    alive = slot_ids[None, :] < block_live[:, None]
    pieces = []
    for target in (-1, 0, 1):
        choose = (block_offsets == target) & alive
        total = jnp.zeros(blocks.shape[:1] + blocks.shape[2:], jnp.float32)
        for m in range(blocks.shape[1]):
            total = total + jnp.where(choose[:, m, None, None], blocks[:, m].astype(jnp.float32), 0.0)
        pieces.append(total.astype(jnp.bfloat16))
    return jnp.stack(pieces, axis=1)


def band_kernel(tile_rows, band_local, half_band, grid_tiles, sent_rows, row_count, col_count):
    extended = band_local + 2
    window = tile_rows + band_local - 1

    def kernel(ids, q_ref, jac_ref, recv_ref, mid_ref, left_ref, right_ref, up_ref, down_ref,
               up_right_ref, down_left_ref, out_ref, win_ref, spread_ref, flipped_ref):
        row_id = ids[0]
        col_id = ids[1]
        first_row = row_id * tile_rows
        low_slot = col_id * band_local - 2
        low_offset = col_id * band_local - half_band
        size = jac_ref.shape[-1]

        for col_value in range(col_count):
            offset = col_value * band_local - half_band

            @pl.when(col_id == col_value)
            def _():
                for position in range(window):
                    at = offset + position
                    for g in range(3):
                        if at < 0:
                            win_ref[position, g] = recv_ref[sent_rows + at, g]
                        elif at < tile_rows:
                            win_ref[position, g] = jac_ref[at, g]
                        else:
                            win_ref[position, g] = recv_ref[at - tile_rows, g]

        def prior_tile(ext_row, ext_slot, masked):
            if ext_slot < 2:
                if ext_row == tile_rows + 1:
                    tile = down_left_ref[band_local - 2 + ext_slot]
                else:
                    tile = left_ref[ext_row - 1, band_local - 2 + ext_slot]
            elif ext_slot >= 2 + band_local:
                if ext_row == 0:
                    tile = up_right_ref[ext_slot - 2 - band_local]
                else:
                    tile = right_ref[ext_row - 1, ext_slot - 2 - band_local]
            elif ext_row == 0:
                tile = up_ref[ext_slot - 2]
            elif ext_row == tile_rows + 1:
                tile = down_ref[ext_slot - 2]
            else:
                tile = mid_ref[ext_row - 1, ext_slot - 2]
            if not masked:
                return tile
            column = first_row + ext_row - 1 + low_slot + ext_slot - half_band
            keep = (column >= 0) & (column < grid_tiles)
            return jnp.where(keep, tile, jnp.zeros_like(tile))

        eye = lax.broadcasted_iota(jnp.int32, (size, size), 0) == lax.broadcasted_iota(
            jnp.int32, (size, size), 1
        )

        def body(masked):
            for ext_row in range(tile_rows + 2):
                for ext_slot in range(extended + 2):
                    used = any(
                        0 <= ext_row - f < tile_rows and 0 <= ext_slot + f - 2 < extended
                        for f in range(3)
                    )
                    if used:
                        flipped_ref[ext_row, ext_slot] = prior_tile(ext_row, ext_slot, masked).T
            for row in range(tile_rows):
                lhs = jnp.concatenate(
                    [
                        jnp.concatenate(
                            [flipped_ref[row + f, u - f + 2] for f in range(3)], axis=1
                        )
                        for u in range(extended)
                    ],
                    axis=0,
                )
                rhs = jnp.concatenate([jac_ref[row, f] for f in range(3)], axis=1)
                spread_ref[row] = lax.dot_general(
                    lhs, rhs, (((1,), (1,)), ((), ())), preferred_element_type=jnp.float32
                ).astype(jnp.bfloat16)
            for position in range(window):
                members = [
                    (position - k, k) for k in range(band_local) if 0 <= position - k < tile_rows
                ]
                left_side = jnp.concatenate([win_ref[position, g] for g in range(3)], axis=1)
                right_side = jnp.concatenate(
                    [spread_ref[row, k * size : (k + 3) * size, :] for row, k in members], axis=1
                )
                product = jnp.dot(left_side, right_side, preferred_element_type=jnp.float32)
                for index, (row, k) in enumerate(members):
                    total = product[:, index * size : (index + 1) * size].T
                    on_diagonal = (low_offset + k == 0).astype(jnp.float32)
                    noise = jnp.where(eye, q_ref[pl.ds(row, 1), :], 0.0)
                    total = total + noise * on_diagonal
                    if masked:
                        column = first_row + row + low_offset + k
                        keep = (column >= 0) & (column < grid_tiles)
                        total = jnp.where(keep, total, jnp.zeros_like(total))
                    out_ref[row, k] = total.astype(out_ref.dtype)

        edge = (row_id == 0) | (row_id == row_count - 1)

        @pl.when(edge)
        def _():
            body(True)

        @pl.when(jnp.logical_not(edge))
        def _():
            body(False)

    return kernel


def shards(p_band, blocks, block_offsets, block_live, q_var):
    tile_rows, band_local, tile_size = p_band.shape[0], p_band.shape[1], p_band.shape[2]
    row_count = lax.axis_size("row")
    col_count = lax.axis_size("col")
    half_band = band_local * col_count // 2
    grid_tiles = tile_rows * row_count
    row_id = lax.axis_index("row")
    col_id = lax.axis_index("col")
    low_offset = col_id * band_local - half_band

    def flat(a, b):
        return a * col_count + b

    left = lax.ppermute(p_band, "col", [(b, b + 1) for b in range(col_count - 1)])
    right = lax.ppermute(p_band, "col", [(b + 1, b) for b in range(col_count - 1)])
    meta = jnp.zeros((tile_size, tile_size), p_band.dtype)
    meta = meta.at[0, : tile_rows * 3].set(block_offsets.reshape(-1).astype(p_band.dtype))
    meta = meta.at[1, :tile_rows].set(block_live.astype(p_band.dtype))
    up_all = lax.ppermute(
        jnp.concatenate([p_band[-1], meta[None]], axis=0), "row", [(a, a + 1) for a in range(row_count - 1)]
    )
    down_all = lax.ppermute(
        jnp.concatenate([p_band[0], meta[None]], axis=0), "row", [(a + 1, a) for a in range(row_count - 1)]
    )
    up = up_all[:band_local]
    down = down_all[:band_local]

    sent_rows = half_band
    lower_half = col_id < col_count // 2
    send_start = jnp.where(lower_half, tile_rows - sent_rows, 0)
    sent = lax.dynamic_slice_in_dim(blocks, send_start, sent_rows, 0)
    pairs = []
    for b in range(col_count):
        if b * band_local - half_band < 0:
            pairs += [(flat(a, b), flat(a + 1, b)) for a in range(row_count - 1)]
        else:
            pairs += [(flat(a, b), flat(a - 1, b)) for a in range(1, row_count)]
    received_blocks = lax.ppermute(sent, ("row", "col"), pairs)

    jacobian = assemble(blocks, block_offsets, block_live)
    received_meta = jnp.where(lower_half, up_all[band_local], down_all[band_local]).astype(jnp.float32)
    received_offsets = jnp.round(received_meta[0, : tile_rows * 3]).astype(jnp.int32).reshape(tile_rows, 3)
    received_live = jnp.round(received_meta[1, :tile_rows]).astype(jnp.int32)
    received = assemble(
        received_blocks,
        lax.dynamic_slice_in_dim(received_offsets, send_start, sent_rows, 0),
        lax.dynamic_slice_in_dim(received_live, send_start, sent_rows, 0),
    )

    down_left = lax.ppermute(down, "col", [(b, b + 1) for b in range(col_count - 1)])
    up_right = lax.ppermute(up, "col", [(b + 1, b) for b in range(col_count - 1)])

    ids = jnp.stack([row_id, col_id]).astype(jnp.int32)
    vmem = pl.BlockSpec(memory_space=pltpu.MemorySpace.VMEM)
    smem = pl.BlockSpec(memory_space=pltpu.MemorySpace.SMEM)
    return pl.pallas_call(
        band_kernel(tile_rows, band_local, half_band, grid_tiles, sent_rows, row_count, col_count),
        out_shape=jax.ShapeDtypeStruct(p_band.shape, p_band.dtype),
        in_specs=[smem] + [vmem] * 10,
        out_specs=vmem,
        scratch_shapes=[
            pltpu.VMEM((tile_rows + band_local - 1, 3, tile_size, tile_size), p_band.dtype),
            pltpu.VMEM((tile_rows, (band_local + 2) * tile_size, tile_size), p_band.dtype),
            pltpu.VMEM((tile_rows + 2, band_local + 4, tile_size, tile_size), p_band.dtype),
        ],
    )(ids, q_var, jacobian, received, p_band, left, right, up, down, up_right, down_left)


def solution(mesh):
    placed = (
        P("row", "col", None, None),
        P("row", None, None, None),
        P("row", None),
        P("row"),
        P("row", None),
    )
    return jax.shard_map(
        shards, mesh=mesh, in_specs=placed, out_specs=P("row", "col", None, None), check_vma=False
    )
```

```python
import jax
import jax.numpy as jnp
from jax import lax
from jax.experimental import pallas as pl
from jax.experimental.pallas import tpu as pltpu
from jax.sharding import PartitionSpec as P


def assemble(blocks, block_offsets, block_live):
    slot_ids = jnp.arange(blocks.shape[1], dtype=jnp.int32)
    alive = slot_ids[None, :] < block_live[:, None]
    pieces = []
    for target in (-1, 0, 1):
        choose = (block_offsets == target) & alive
        total = jnp.zeros(blocks.shape[:1] + blocks.shape[2:], jnp.float32)
        for m in range(blocks.shape[1]):
            total = total + jnp.where(choose[:, m, None, None], blocks[:, m].astype(jnp.float32), 0.0)
        pieces.append(total.astype(jnp.bfloat16))
    return jnp.stack(pieces, axis=1)


def band_kernel(tile_rows, band_local, half_band, grid_tiles, sent_rows, row_count, col_count):
    extended = band_local + 2
    window = tile_rows + band_local - 1

    def kernel(ids, q_ref, jac_ref, recv_ref, mid_ref, left_ref, right_ref, up_ref, down_ref,
               up_right_ref, down_left_ref, out_ref, win_ref, spread_ref, flipped_ref):
        row_id = ids[0]
        col_id = ids[1]
        first_row = row_id * tile_rows
        low_slot = col_id * band_local - 2
        low_offset = col_id * band_local - half_band
        size = jac_ref.shape[-1]

        for col_value in range(col_count):
            offset = col_value * band_local - half_band

            @pl.when(col_id == col_value)
            def _():
                for position in range(window):
                    at = offset + position
                    for g in range(3):
                        if at < 0:
                            win_ref[position, g] = recv_ref[sent_rows + at, g]
                        elif at < tile_rows:
                            win_ref[position, g] = jac_ref[at, g]
                        else:
                            win_ref[position, g] = recv_ref[at - tile_rows, g]

        def prior_tile(ext_row, ext_slot, masked):
            if ext_slot < 2:
                if ext_row == tile_rows + 1:
                    tile = down_left_ref[band_local - 2 + ext_slot]
                else:
                    tile = left_ref[ext_row - 1, band_local - 2 + ext_slot]
            elif ext_slot >= 2 + band_local:
                if ext_row == 0:
                    tile = up_right_ref[ext_slot - 2 - band_local]
                else:
                    tile = right_ref[ext_row - 1, ext_slot - 2 - band_local]
            elif ext_row == 0:
                tile = up_ref[ext_slot - 2]
            elif ext_row == tile_rows + 1:
                tile = down_ref[ext_slot - 2]
            else:
                tile = mid_ref[ext_row - 1, ext_slot - 2]
            if not masked:
                return tile
            column = first_row + ext_row - 1 + low_slot + ext_slot - half_band
            keep = (column >= 0) & (column < grid_tiles)
            return jnp.where(keep, tile, jnp.zeros_like(tile))

        eye = lax.broadcasted_iota(jnp.int32, (size, size), 0) == lax.broadcasted_iota(
            jnp.int32, (size, size), 1
        )

        def body(masked):
            for ext_row in range(tile_rows + 2):
                for ext_slot in range(extended + 2):
                    used = any(
                        0 <= ext_row - f < tile_rows and 0 <= ext_slot + f - 2 < extended
                        for f in range(3)
                    )
                    if used:
                        flipped_ref[ext_row, ext_slot] = prior_tile(ext_row, ext_slot, masked).T
            for row in range(tile_rows):
                lhs = jnp.concatenate(
                    [
                        jnp.concatenate(
                            [flipped_ref[row + f, u - f + 2] for f in range(3)], axis=1
                        )
                        for u in range(extended)
                    ],
                    axis=0,
                )
                rhs = jnp.concatenate([jac_ref[row, f] for f in range(3)], axis=1)
                flipped_spread = lax.dot_general(
                    lhs, rhs, (((1,), (1,)), ((), ())), preferred_element_type=jnp.float32
                ).astype(jnp.bfloat16)
                for u in range(extended):
                    spread_ref[row, :, u * size : (u + 1) * size] = flipped_spread[
                        u * size : (u + 1) * size
                    ].T
            for position in range(window):
                members = [
                    (position - k, k) for k in range(band_local) if 0 <= position - k < tile_rows
                ]
                left_side = jnp.concatenate(
                    [spread_ref[row, :, k * size : (k + 3) * size] for row, k in members], axis=0
                )
                right_side = jnp.concatenate([win_ref[position, g] for g in range(3)], axis=1)
                product = lax.dot_general(
                    left_side,
                    right_side,
                    (((1,), (1,)), ((), ())),
                    preferred_element_type=jnp.float32,
                )
                for index, (row, k) in enumerate(members):
                    total = product[index * size : (index + 1) * size]
                    on_diagonal = (low_offset + k == 0).astype(jnp.float32)
                    noise = jnp.where(eye, q_ref[pl.ds(row, 1), :], 0.0)
                    total = total + noise * on_diagonal
                    if masked:
                        column = first_row + row + low_offset + k
                        keep = (column >= 0) & (column < grid_tiles)
                        total = jnp.where(keep, total, jnp.zeros_like(total))
                    out_ref[row, k] = total.astype(out_ref.dtype)

        edge = (row_id == 0) | (row_id == row_count - 1)

        @pl.when(edge)
        def _():
            body(True)

        @pl.when(jnp.logical_not(edge))
        def _():
            body(False)

    return kernel


def shards(p_band, blocks, block_offsets, block_live, q_var):
    tile_rows, band_local, tile_size = p_band.shape[0], p_band.shape[1], p_band.shape[2]
    row_count = lax.axis_size("row")
    col_count = lax.axis_size("col")
    half_band = band_local * col_count // 2
    grid_tiles = tile_rows * row_count
    row_id = lax.axis_index("row")
    col_id = lax.axis_index("col")
    low_offset = col_id * band_local - half_band

    def flat(a, b):
        return a * col_count + b

    left = lax.ppermute(p_band, "col", [(b, b + 1) for b in range(col_count - 1)])
    right = lax.ppermute(p_band, "col", [(b + 1, b) for b in range(col_count - 1)])
    meta = jnp.zeros((tile_size, tile_size), p_band.dtype)
    meta = meta.at[0, : tile_rows * 3].set(block_offsets.reshape(-1).astype(p_band.dtype))
    meta = meta.at[1, :tile_rows].set(block_live.astype(p_band.dtype))
    up_all = lax.ppermute(
        jnp.concatenate([p_band[-1], meta[None]], axis=0), "row", [(a, a + 1) for a in range(row_count - 1)]
    )
    down_all = lax.ppermute(
        jnp.concatenate([p_band[0], meta[None]], axis=0), "row", [(a + 1, a) for a in range(row_count - 1)]
    )
    up = up_all[:band_local]
    down = down_all[:band_local]

    sent_rows = half_band
    lower_half = col_id < col_count // 2
    send_start = jnp.where(lower_half, tile_rows - sent_rows, 0)
    sent = lax.dynamic_slice_in_dim(blocks, send_start, sent_rows, 0)
    pairs = []
    for b in range(col_count):
        if b * band_local - half_band < 0:
            pairs += [(flat(a, b), flat(a + 1, b)) for a in range(row_count - 1)]
        else:
            pairs += [(flat(a, b), flat(a - 1, b)) for a in range(1, row_count)]
    received_blocks = lax.ppermute(sent, ("row", "col"), pairs)

    jacobian = assemble(blocks, block_offsets, block_live)
    received_meta = jnp.where(lower_half, up_all[band_local], down_all[band_local]).astype(jnp.float32)
    received_offsets = jnp.round(received_meta[0, : tile_rows * 3]).astype(jnp.int32).reshape(tile_rows, 3)
    received_live = jnp.round(received_meta[1, :tile_rows]).astype(jnp.int32)
    received = assemble(
        received_blocks,
        lax.dynamic_slice_in_dim(received_offsets, send_start, sent_rows, 0),
        lax.dynamic_slice_in_dim(received_live, send_start, sent_rows, 0),
    )

    down_left = lax.ppermute(down, "col", [(b, b + 1) for b in range(col_count - 1)])
    up_right = lax.ppermute(up, "col", [(b + 1, b) for b in range(col_count - 1)])

    ids = jnp.stack([row_id, col_id]).astype(jnp.int32)
    vmem = pl.BlockSpec(memory_space=pltpu.MemorySpace.VMEM)
    smem = pl.BlockSpec(memory_space=pltpu.MemorySpace.SMEM)
    return pl.pallas_call(
        band_kernel(tile_rows, band_local, half_band, grid_tiles, sent_rows, row_count, col_count),
        out_shape=jax.ShapeDtypeStruct(p_band.shape, p_band.dtype),
        in_specs=[smem] + [vmem] * 10,
        out_specs=vmem,
        scratch_shapes=[
            pltpu.VMEM((tile_rows + band_local - 1, 3, tile_size, tile_size), p_band.dtype),
            pltpu.VMEM((tile_rows, tile_size, (band_local + 2) * tile_size), p_band.dtype),
            pltpu.VMEM((tile_rows + 2, band_local + 4, tile_size, tile_size), p_band.dtype),
        ],
    )(ids, q_var, jacobian, received, p_band, left, right, up, down, up_right, down_left)


def solution(mesh):
    placed = (
        P("row", "col", None, None),
        P("row", None, None, None),
        P("row", None),
        P("row"),
        P("row", None),
    )
    return jax.shard_map(
        shards, mesh=mesh, in_specs=placed, out_specs=P("row", "col", None, None), check_vma=False
    )
```

```python
import jax
import jax.numpy as jnp
from jax import lax
from jax.experimental import pallas as pl
from jax.experimental.pallas import tpu as pltpu
from jax.sharding import PartitionSpec as P


def assemble(blocks, block_offsets, block_live):
    slot_ids = jnp.arange(blocks.shape[1], dtype=jnp.int32)
    alive = slot_ids[None, :] < block_live[:, None]
    pieces = []
    for target in (-1, 0, 1):
        choose = (block_offsets == target) & alive
        total = jnp.zeros(blocks.shape[:1] + blocks.shape[2:], jnp.float32)
        for m in range(blocks.shape[1]):
            total = total + jnp.where(choose[:, m, None, None], blocks[:, m].astype(jnp.float32), 0.0)
        pieces.append(total.astype(jnp.bfloat16))
    return jnp.stack(pieces, axis=1)


def band_kernel(tile_rows, band_local, half_band, grid_tiles, sent_rows, row_count, col_count):
    extended = band_local + 2
    window = tile_rows + band_local - 1

    def kernel(ids, q_ref, jac_ref, recv_ref, mid_ref, left_ref, right_ref, up_ref, down_ref,
               up_right_ref, down_left_ref, out_ref, win_ref, spread_ref):
        row_id = ids[0]
        col_id = ids[1]
        first_row = row_id * tile_rows
        low_slot = col_id * band_local - 2
        low_offset = col_id * band_local - half_band
        size = jac_ref.shape[-1]

        for col_value in range(col_count):
            offset = col_value * band_local - half_band

            @pl.when(col_id == col_value)
            def _():
                for position in range(window):
                    at = offset + position
                    for g in range(3):
                        if at < 0:
                            win_ref[position, g] = recv_ref[sent_rows + at, g]
                        elif at < tile_rows:
                            win_ref[position, g] = jac_ref[at, g]
                        else:
                            win_ref[position, g] = recv_ref[at - tile_rows, g]

        def prior_tile(ext_row, ext_slot, masked):
            if ext_slot < 2:
                if ext_row == tile_rows + 1:
                    tile = down_left_ref[band_local - 2 + ext_slot]
                else:
                    tile = left_ref[ext_row - 1, band_local - 2 + ext_slot]
            elif ext_slot >= 2 + band_local:
                if ext_row == 0:
                    tile = up_right_ref[ext_slot - 2 - band_local]
                else:
                    tile = right_ref[ext_row - 1, ext_slot - 2 - band_local]
            elif ext_row == 0:
                tile = up_ref[ext_slot - 2]
            elif ext_row == tile_rows + 1:
                tile = down_ref[ext_slot - 2]
            else:
                tile = mid_ref[ext_row - 1, ext_slot - 2]
            if not masked:
                return tile
            column = first_row + ext_row - 1 + low_slot + ext_slot - half_band
            keep = (column >= 0) & (column < grid_tiles)
            return jnp.where(keep, tile, jnp.zeros_like(tile))

        eye = lax.broadcasted_iota(jnp.int32, (size, size), 0) == lax.broadcasted_iota(
            jnp.int32, (size, size), 1
        )

        def body(masked):
            for row in range(tile_rows):
                lhs = jnp.concatenate([jac_ref[row, f] for f in range(3)], axis=1)
                rhs = jnp.concatenate(
                    [
                        jnp.concatenate(
                            [prior_tile(row + f, u - f + 2, masked) for u in range(extended)], axis=1
                        )
                        for f in range(3)
                    ],
                    axis=0,
                )
                spread_ref[row] = jnp.dot(lhs, rhs, preferred_element_type=jnp.float32).astype(
                    jnp.bfloat16
                )
            for position in range(window):
                members = [
                    (position - k, k) for k in range(band_local) if 0 <= position - k < tile_rows
                ]
                left_side = jnp.concatenate(
                    [spread_ref[row, :, k * size : (k + 3) * size] for row, k in members], axis=0
                )
                right_side = jnp.concatenate([win_ref[position, g] for g in range(3)], axis=1)
                product = lax.dot_general(
                    left_side,
                    right_side,
                    (((1,), (1,)), ((), ())),
                    preferred_element_type=jnp.float32,
                )
                for index, (row, k) in enumerate(members):
                    total = product[index * size : (index + 1) * size]
                    on_diagonal = (low_offset + k == 0).astype(jnp.float32)
                    noise = jnp.where(eye, q_ref[pl.ds(row, 1), :], 0.0)
                    total = total + noise * on_diagonal
                    if masked:
                        column = first_row + row + low_offset + k
                        keep = (column >= 0) & (column < grid_tiles)
                        total = jnp.where(keep, total, jnp.zeros_like(total))
                    out_ref[row, k] = total.astype(out_ref.dtype)

        edge = (row_id == 0) | (row_id == row_count - 1)

        @pl.when(edge)
        def _():
            body(True)

        @pl.when(jnp.logical_not(edge))
        def _():
            body(False)

    return kernel


def shards(p_band, blocks, block_offsets, block_live, q_var):
    tile_rows, band_local, tile_size = p_band.shape[0], p_band.shape[1], p_band.shape[2]
    row_count = lax.axis_size("row")
    col_count = lax.axis_size("col")
    half_band = band_local * col_count // 2
    grid_tiles = tile_rows * row_count
    row_id = lax.axis_index("row")
    col_id = lax.axis_index("col")
    low_offset = col_id * band_local - half_band

    def flat(a, b):
        return a * col_count + b

    left = lax.ppermute(p_band, "col", [(b, b + 1) for b in range(col_count - 1)])
    right = lax.ppermute(p_band, "col", [(b + 1, b) for b in range(col_count - 1)])
    up = lax.ppermute(p_band[-1], "row", [(a, a + 1) for a in range(row_count - 1)])
    down = lax.ppermute(p_band[0], "row", [(a + 1, a) for a in range(row_count - 1)])

    sent_rows = half_band
    lower_half = col_id < col_count // 2
    send_start = jnp.where(lower_half, tile_rows - sent_rows, 0)
    sent_offsets = lax.dynamic_slice_in_dim(block_offsets, send_start, sent_rows, 0)
    sent_live = lax.dynamic_slice_in_dim(block_live, send_start, sent_rows, 0)
    meta = jnp.zeros((tile_size, tile_size), blocks.dtype)
    meta = meta.at[0, : sent_rows * 3].set(sent_offsets.reshape(-1).astype(blocks.dtype))
    meta = meta.at[1, :sent_rows].set(sent_live.astype(blocks.dtype))
    sent_tiles = lax.dynamic_slice_in_dim(blocks, send_start, sent_rows, 0).reshape(
        (sent_rows * 3, tile_size, tile_size)
    )
    sent = jnp.concatenate([sent_tiles, meta[None]], axis=0)
    pairs = []
    for b in range(col_count):
        if b * band_local - half_band < 0:
            pairs += [(flat(a, b), flat(a + 1, b)) for a in range(row_count - 1)]
        else:
            pairs += [(flat(a, b), flat(a - 1, b)) for a in range(1, row_count)]
    received_all = lax.ppermute(sent, ("row", "col"), pairs)

    jacobian = assemble(blocks, block_offsets, block_live)
    received_meta = received_all[sent_rows * 3].astype(jnp.float32)
    received = assemble(
        received_all[: sent_rows * 3].reshape((sent_rows, 3, tile_size, tile_size)),
        jnp.round(received_meta[0, : sent_rows * 3]).astype(jnp.int32).reshape(sent_rows, 3),
        jnp.round(received_meta[1, :sent_rows]).astype(jnp.int32),
    )

    down_left = lax.ppermute(down, "col", [(b, b + 1) for b in range(col_count - 1)])
    up_right = lax.ppermute(up, "col", [(b + 1, b) for b in range(col_count - 1)])

    ids = jnp.stack([row_id, col_id]).astype(jnp.int32)
    vmem = pl.BlockSpec(memory_space=pltpu.MemorySpace.VMEM)
    smem = pl.BlockSpec(memory_space=pltpu.MemorySpace.SMEM)
    return pl.pallas_call(
        band_kernel(tile_rows, band_local, half_band, grid_tiles, sent_rows, row_count, col_count),
        out_shape=jax.ShapeDtypeStruct(p_band.shape, p_band.dtype),
        in_specs=[smem] + [vmem] * 10,
        out_specs=vmem,
        scratch_shapes=[
            pltpu.VMEM((tile_rows + band_local - 1, 3, tile_size, tile_size), p_band.dtype),
            pltpu.VMEM((tile_rows, tile_size, (band_local + 2) * tile_size), p_band.dtype),
        ],
    )(ids, q_var, jacobian, received, p_band, left, right, up, down, up_right, down_left)


def solution(mesh):
    placed = (
        P("row", "col", None, None),
        P("row", None, None, None),
        P("row", None),
        P("row"),
        P("row", None),
    )
    return jax.shard_map(
        shards, mesh=mesh, in_specs=placed, out_specs=P("row", "col", None, None), check_vma=False
    )
```

```python
import jax
import jax.numpy as jnp
from jax import lax
from jax.experimental import pallas as pl
from jax.experimental.pallas import tpu as pltpu
from jax.sharding import PartitionSpec as P


def assemble(blocks, block_offsets, block_live):
    slot_ids = jnp.arange(blocks.shape[1], dtype=jnp.int32)
    alive = slot_ids[None, :] < block_live[:, None]
    pieces = []
    for target in (-1, 0, 1):
        choose = (block_offsets == target) & alive
        total = jnp.zeros(blocks.shape[:1] + blocks.shape[2:], jnp.float32)
        for m in range(blocks.shape[1]):
            total = total + jnp.where(choose[:, m, None, None], blocks[:, m].astype(jnp.float32), 0.0)
        pieces.append(total.astype(jnp.bfloat16))
    return jnp.stack(pieces, axis=1)


def band_kernel(tile_rows, band_local, half_band, grid_tiles, sent_rows, row_count, col_count, inner):
    extended = band_local + 2
    window = tile_rows + band_local - 1
    inner_rows = range(1, tile_rows - 1)

    def inner_kernel(ids, jac_ref, mid_ref, left_ref, right_ref, out_ref):
        kernel(ids, None, jac_ref, None, mid_ref, left_ref, right_ref, None, None, None, None, None,
               out_ref, None, None)

    def final_kernel(ids, q_ref, jac_ref, recv_ref, mid_ref, left_ref, right_ref, up_ref, down_ref,
                     up_right_ref, down_left_ref, inner_ref, out_ref, win_ref, spread_ref):
        kernel(ids, q_ref, jac_ref, recv_ref, mid_ref, left_ref, right_ref, up_ref, down_ref,
               up_right_ref, down_left_ref, inner_ref, out_ref, win_ref, spread_ref)

    def kernel(ids, q_ref, jac_ref, recv_ref, mid_ref, left_ref, right_ref, up_ref, down_ref,
               up_right_ref, down_left_ref, inner_ref, out_ref, win_ref, spread_ref):
        row_id = ids[0]
        col_id = ids[1]
        first_row = row_id * tile_rows
        low_slot = col_id * band_local - 2
        low_offset = col_id * band_local - half_band
        size = jac_ref.shape[-1]

        for col_value in range(0 if inner else col_count):
            offset = col_value * band_local - half_band

            @pl.when(col_id == col_value)
            def _():
                for position in range(window):
                    at = offset + position
                    for g in range(3):
                        if at < 0:
                            win_ref[position, g] = recv_ref[sent_rows + at, g]
                        elif at < tile_rows:
                            win_ref[position, g] = jac_ref[at, g]
                        else:
                            win_ref[position, g] = recv_ref[at - tile_rows, g]

        def prior_tile(ext_row, ext_slot, masked):
            if ext_slot < 2:
                if ext_row == tile_rows + 1:
                    tile = down_left_ref[band_local - 2 + ext_slot]
                else:
                    tile = left_ref[ext_row - 1, band_local - 2 + ext_slot]
            elif ext_slot >= 2 + band_local:
                if ext_row == 0:
                    tile = up_right_ref[ext_slot - 2 - band_local]
                else:
                    tile = right_ref[ext_row - 1, ext_slot - 2 - band_local]
            elif ext_row == 0:
                tile = up_ref[ext_slot - 2]
            elif ext_row == tile_rows + 1:
                tile = down_ref[ext_slot - 2]
            else:
                tile = mid_ref[ext_row - 1, ext_slot - 2]
            if not masked:
                return tile
            column = first_row + ext_row - 1 + low_slot + ext_slot - half_band
            keep = (column >= 0) & (column < grid_tiles)
            return jnp.where(keep, tile, jnp.zeros_like(tile))

        eye = lax.broadcasted_iota(jnp.int32, (size, size), 0) == lax.broadcasted_iota(
            jnp.int32, (size, size), 1
        )

        def spread_rows(row):
            if inner:
                return out_ref.at[row - 1]
            if row in inner_rows:
                return inner_ref.at[row - 1]
            return spread_ref.at[row]

        def body(masked):
            for row in range(tile_rows):
                if (row in inner_rows) != inner:
                    continue
                lhs = jnp.concatenate([jac_ref[row, f] for f in range(3)], axis=1)
                rhs = jnp.concatenate(
                    [
                        jnp.concatenate(
                            [prior_tile(row + f, u - f + 2, masked) for u in range(extended)], axis=1
                        )
                        for f in range(3)
                    ],
                    axis=0,
                )
                spread_rows(row)[...] = jnp.dot(lhs, rhs, preferred_element_type=jnp.float32).astype(
                    jnp.bfloat16
                )
            if inner:
                return
            for position in range(window):
                members = [
                    (position - k, k) for k in range(band_local) if 0 <= position - k < tile_rows
                ]
                left_side = jnp.concatenate(
                    [spread_rows(row)[:, k * size : (k + 3) * size] for row, k in members], axis=0
                )
                right_side = jnp.concatenate([win_ref[position, g] for g in range(3)], axis=1)
                product = lax.dot_general(
                    left_side,
                    right_side,
                    (((1,), (1,)), ((), ())),
                    preferred_element_type=jnp.float32,
                )
                for index, (row, k) in enumerate(members):
                    total = product[index * size : (index + 1) * size]
                    on_diagonal = (low_offset + k == 0).astype(jnp.float32)
                    noise = jnp.where(eye, q_ref[pl.ds(row, 1), :], 0.0)
                    total = total + noise * on_diagonal
                    if masked:
                        column = first_row + row + low_offset + k
                        keep = (column >= 0) & (column < grid_tiles)
                        total = jnp.where(keep, total, jnp.zeros_like(total))
                    out_ref[row, k] = total.astype(out_ref.dtype)

        edge = (row_id == 0) | (row_id == row_count - 1)

        @pl.when(edge)
        def _():
            body(True)

        @pl.when(jnp.logical_not(edge))
        def _():
            body(False)

    return inner_kernel if inner else final_kernel


def shards(p_band, blocks, block_offsets, block_live, q_var):
    tile_rows, band_local, tile_size = p_band.shape[0], p_band.shape[1], p_band.shape[2]
    row_count = lax.axis_size("row")
    col_count = lax.axis_size("col")
    half_band = band_local * col_count // 2
    grid_tiles = tile_rows * row_count
    row_id = lax.axis_index("row")
    col_id = lax.axis_index("col")
    low_offset = col_id * band_local - half_band

    def flat(a, b):
        return a * col_count + b

    left = lax.ppermute(p_band, "col", [(b, b + 1) for b in range(col_count - 1)])
    right = lax.ppermute(p_band, "col", [(b + 1, b) for b in range(col_count - 1)])
    up = lax.ppermute(p_band[-1], "row", [(a, a + 1) for a in range(row_count - 1)])
    down = lax.ppermute(p_band[0], "row", [(a + 1, a) for a in range(row_count - 1)])

    sent_rows = half_band
    lower_half = col_id < col_count // 2
    send_start = jnp.where(lower_half, tile_rows - sent_rows, 0)
    sent_offsets = lax.dynamic_slice_in_dim(block_offsets, send_start, sent_rows, 0)
    sent_live = lax.dynamic_slice_in_dim(block_live, send_start, sent_rows, 0)
    meta = jnp.zeros((tile_size, tile_size), blocks.dtype)
    meta = meta.at[0, : sent_rows * 3].set(sent_offsets.reshape(-1).astype(blocks.dtype))
    meta = meta.at[1, :sent_rows].set(sent_live.astype(blocks.dtype))
    sent_tiles = lax.dynamic_slice_in_dim(blocks, send_start, sent_rows, 0).reshape(
        (sent_rows * 3, tile_size, tile_size)
    )
    sent = jnp.concatenate([sent_tiles, meta[None]], axis=0)
    pairs = []
    for b in range(col_count):
        if b * band_local - half_band < 0:
            pairs += [(flat(a, b), flat(a + 1, b)) for a in range(row_count - 1)]
        else:
            pairs += [(flat(a, b), flat(a - 1, b)) for a in range(1, row_count)]
    received_all = lax.ppermute(sent, ("row", "col"), pairs)

    jacobian = assemble(blocks, block_offsets, block_live)
    received_meta = received_all[sent_rows * 3].astype(jnp.float32)
    received = assemble(
        received_all[: sent_rows * 3].reshape((sent_rows, 3, tile_size, tile_size)),
        jnp.round(received_meta[0, : sent_rows * 3]).astype(jnp.int32).reshape(sent_rows, 3),
        jnp.round(received_meta[1, :sent_rows]).astype(jnp.int32),
    )

    down_left = lax.ppermute(down, "col", [(b, b + 1) for b in range(col_count - 1)])
    up_right = lax.ppermute(up, "col", [(b + 1, b) for b in range(col_count - 1)])

    ids = jnp.stack([row_id, col_id]).astype(jnp.int32)
    vmem = pl.BlockSpec(memory_space=pltpu.MemorySpace.VMEM)
    smem = pl.BlockSpec(memory_space=pltpu.MemorySpace.SMEM)
    sizes = (tile_rows, band_local, half_band, grid_tiles, sent_rows, row_count, col_count)
    spread_row = (tile_size, (band_local + 2) * tile_size)
    inner_spread = pl.pallas_call(
        band_kernel(*sizes, True),
        out_shape=jax.ShapeDtypeStruct((tile_rows - 2,) + spread_row, p_band.dtype),
        in_specs=[smem] + [vmem] * 4,
        out_specs=vmem,
    )(ids, jacobian, p_band, left, right)
    return pl.pallas_call(
        band_kernel(*sizes, False),
        out_shape=jax.ShapeDtypeStruct(p_band.shape, p_band.dtype),
        in_specs=[smem] + [vmem] * 11,
        out_specs=vmem,
        scratch_shapes=[
            pltpu.VMEM((tile_rows + band_local - 1, 3, tile_size, tile_size), p_band.dtype),
            pltpu.VMEM((tile_rows,) + spread_row, p_band.dtype),
        ],
    )(ids, q_var, jacobian, received, p_band, left, right, up, down, up_right, down_left, inner_spread)


def solution(mesh):
    placed = (
        P("row", "col", None, None),
        P("row", None, None, None),
        P("row", None),
        P("row"),
        P("row", None),
    )
    return jax.shard_map(
        shards, mesh=mesh, in_specs=placed, out_specs=P("row", "col", None, None), check_vma=False
    )
```

```python
import jax
import jax.numpy as jnp
from jax import lax
from jax.experimental import pallas as pl
from jax.experimental.pallas import tpu as pltpu
from jax.sharding import PartitionSpec as P


def assemble(blocks, block_offsets, block_live):
    slot_ids = jnp.arange(blocks.shape[1], dtype=jnp.int32)
    alive = slot_ids[None, :] < block_live[:, None]
    pieces = []
    for target in (-1, 0, 1):
        choose = (block_offsets == target) & alive
        total = jnp.zeros(blocks.shape[:1] + blocks.shape[2:], jnp.float32)
        for m in range(blocks.shape[1]):
            total = total + jnp.where(choose[:, m, None, None], blocks[:, m].astype(jnp.float32), 0.0)
        pieces.append(total.astype(jnp.bfloat16))
    return jnp.stack(pieces, axis=1)


def band_kernel(tile_rows, band_local, half_band, grid_tiles, sent_rows, row_count, col_count):
    extended = band_local + 2
    window = tile_rows + band_local - 1

    half_rows = tile_rows // 2

    def kernel(ids, q_ref, jac_ref, recv_ref, mid_ref, left_ref, left_late_ref, right_ref,
               right_late_ref, up_ref, down_ref, out_ref, win_ref, spread_ref):
        row_id = ids[0]
        col_id = ids[1]
        first_row = row_id * tile_rows
        low_slot = col_id * band_local - 2
        low_offset = col_id * band_local - half_band
        size = jac_ref.shape[-1]

        for col_value in range(col_count):
            offset = col_value * band_local - half_band

            @pl.when(col_id == col_value)
            def _():
                for position in range(window):
                    at = offset + position
                    for g in range(3):
                        if at < 0:
                            win_ref[position, g] = recv_ref[sent_rows + at, g]
                        elif at < tile_rows:
                            win_ref[position, g] = jac_ref[at, g]
                        else:
                            win_ref[position, g] = recv_ref[at - tile_rows, g]

        def prior_tile(ext_row, ext_slot, masked):
            at = ext_row - 1
            if ext_slot < 2:
                if at < half_rows:
                    tile = left_ref[at, band_local - 2 + ext_slot]
                else:
                    tile = left_late_ref[at - half_rows, band_local - 2 + ext_slot]
            elif ext_slot >= 2 + band_local:
                if 0 <= at < half_rows:
                    tile = right_ref[at, ext_slot - 2 - band_local]
                else:
                    tile = right_late_ref[max(at - half_rows + 1, 0), ext_slot - 2 - band_local]
            elif ext_row == 0:
                tile = up_ref[ext_slot - 2]
            elif ext_row == tile_rows + 1:
                tile = down_ref[ext_slot - 2]
            else:
                tile = mid_ref[ext_row - 1, ext_slot - 2]
            if not masked:
                return tile
            column = first_row + ext_row - 1 + low_slot + ext_slot - half_band
            keep = (column >= 0) & (column < grid_tiles)
            return jnp.where(keep, tile, jnp.zeros_like(tile))

        eye = lax.broadcasted_iota(jnp.int32, (size, size), 0) == lax.broadcasted_iota(
            jnp.int32, (size, size), 1
        )

        def body(masked):
            for row in range(tile_rows):
                lhs = jnp.concatenate([jac_ref[row, f] for f in range(3)], axis=1)
                rhs = jnp.concatenate(
                    [
                        jnp.concatenate(
                            [prior_tile(row + f, u - f + 2, masked) for u in range(extended)], axis=1
                        )
                        for f in range(3)
                    ],
                    axis=0,
                )
                spread_ref[row] = jnp.dot(lhs, rhs, preferred_element_type=jnp.float32).astype(
                    jnp.bfloat16
                )
            for position in range(window):
                members = [
                    (position - k, k) for k in range(band_local) if 0 <= position - k < tile_rows
                ]
                left_side = jnp.concatenate(
                    [spread_ref[row, :, k * size : (k + 3) * size] for row, k in members], axis=0
                )
                right_side = jnp.concatenate([win_ref[position, g] for g in range(3)], axis=1)
                product = lax.dot_general(
                    left_side,
                    right_side,
                    (((1,), (1,)), ((), ())),
                    preferred_element_type=jnp.float32,
                )
                for index, (row, k) in enumerate(members):
                    total = product[index * size : (index + 1) * size]
                    on_diagonal = (low_offset + k == 0).astype(jnp.float32)
                    noise = jnp.where(eye, q_ref[pl.ds(row, 1), :], 0.0)
                    total = total + noise * on_diagonal
                    if masked:
                        column = first_row + row + low_offset + k
                        keep = (column >= 0) & (column < grid_tiles)
                        total = jnp.where(keep, total, jnp.zeros_like(total))
                    out_ref[row, k] = total.astype(out_ref.dtype)

        edge = (row_id == 0) | (row_id == row_count - 1)

        @pl.when(edge)
        def _():
            body(True)

        @pl.when(jnp.logical_not(edge))
        def _():
            body(False)

    return kernel


def shards(p_band, blocks, block_offsets, block_live, q_var):
    tile_rows, band_local, tile_size = p_band.shape[0], p_band.shape[1], p_band.shape[2]
    row_count = lax.axis_size("row")
    col_count = lax.axis_size("col")
    half_band = band_local * col_count // 2
    grid_tiles = tile_rows * row_count
    row_id = lax.axis_index("row")
    col_id = lax.axis_index("col")
    low_offset = col_id * band_local - half_band

    def flat(a, b):
        return a * col_count + b

    half_rows = tile_rows // 2
    early = p_band[:half_rows]
    left = lax.ppermute(early, "col", [(b, b + 1) for b in range(col_count - 1)])
    right = lax.ppermute(early, "col", [(b + 1, b) for b in range(col_count - 1)])
    up = lax.ppermute(p_band[-1], "row", [(a, a + 1) for a in range(row_count - 1)])
    down = lax.ppermute(p_band[0], "row", [(a + 1, a) for a in range(row_count - 1)])

    sent_rows = half_band
    lower_half = col_id < col_count // 2
    send_start = jnp.where(lower_half, tile_rows - sent_rows, 0)
    sent_offsets = lax.dynamic_slice_in_dim(block_offsets, send_start, sent_rows, 0)
    sent_live = lax.dynamic_slice_in_dim(block_live, send_start, sent_rows, 0)
    meta = jnp.zeros((tile_size, tile_size), blocks.dtype)
    meta = meta.at[0, : sent_rows * 3].set(sent_offsets.reshape(-1).astype(blocks.dtype))
    meta = meta.at[1, :sent_rows].set(sent_live.astype(blocks.dtype))
    sent_tiles = lax.dynamic_slice_in_dim(blocks, send_start, sent_rows, 0).reshape(
        (sent_rows * 3, tile_size, tile_size)
    )
    sent = jnp.concatenate([sent_tiles, meta[None]], axis=0)
    pairs = []
    for b in range(col_count):
        if b * band_local - half_band < 0:
            pairs += [(flat(a, b), flat(a + 1, b)) for a in range(row_count - 1)]
        else:
            pairs += [(flat(a, b), flat(a - 1, b)) for a in range(1, row_count)]
    received_all = lax.ppermute(sent, ("row", "col"), pairs)

    jacobian = assemble(blocks, block_offsets, block_live)
    received_meta = received_all[sent_rows * 3].astype(jnp.float32)
    received = assemble(
        received_all[: sent_rows * 3].reshape((sent_rows, 3, tile_size, tile_size)),
        jnp.round(received_meta[0, : sent_rows * 3]).astype(jnp.int32).reshape(sent_rows, 3),
        jnp.round(received_meta[1, :sent_rows]).astype(jnp.int32),
    )

    left_late = lax.ppermute(
        jnp.concatenate([p_band[half_rows:], down[None]], axis=0),
        "col",
        [(b, b + 1) for b in range(col_count - 1)],
    )
    right_late = lax.ppermute(
        jnp.concatenate([up[None], p_band[half_rows:]], axis=0),
        "col",
        [(b + 1, b) for b in range(col_count - 1)],
    )

    ids = jnp.stack([row_id, col_id]).astype(jnp.int32)
    vmem = pl.BlockSpec(memory_space=pltpu.MemorySpace.VMEM)
    smem = pl.BlockSpec(memory_space=pltpu.MemorySpace.SMEM)
    return pl.pallas_call(
        band_kernel(tile_rows, band_local, half_band, grid_tiles, sent_rows, row_count, col_count),
        out_shape=jax.ShapeDtypeStruct(p_band.shape, p_band.dtype),
        in_specs=[smem] + [vmem] * 10,
        out_specs=vmem,
        scratch_shapes=[
            pltpu.VMEM((tile_rows + band_local - 1, 3, tile_size, tile_size), p_band.dtype),
            pltpu.VMEM((tile_rows, tile_size, (band_local + 2) * tile_size), p_band.dtype),
        ],
    )(ids, q_var, jacobian, received, p_band, left, left_late, right, right_late, up, down)


def solution(mesh):
    placed = (
        P("row", "col", None, None),
        P("row", None, None, None),
        P("row", None),
        P("row"),
        P("row", None),
    )
    return jax.shard_map(
        shards, mesh=mesh, in_specs=placed, out_specs=P("row", "col", None, None), check_vma=False
    )
```

```python
import jax
import jax.numpy as jnp
from jax import lax
from jax.experimental import pallas as pl
from jax.experimental.pallas import tpu as pltpu
from jax.sharding import PartitionSpec as P


def assemble(blocks, block_offsets, block_live):
    slot_ids = jnp.arange(blocks.shape[1], dtype=jnp.int32)
    alive = slot_ids[None, :] < block_live[:, None]
    pieces = []
    for target in (-1, 0, 1):
        choose = (block_offsets == target) & alive
        total = jnp.zeros(blocks.shape[:1] + blocks.shape[2:], jnp.float32)
        for m in range(blocks.shape[1]):
            total = total + jnp.where(choose[:, m, None, None], blocks[:, m].astype(jnp.float32), 0.0)
        pieces.append(total.astype(jnp.bfloat16))
    return jnp.stack(pieces, axis=1)


def band_kernel(tile_rows, band_local, half_band, grid_tiles, sent_rows, row_count, col_count):
    extended = band_local + 2
    window = tile_rows + band_local - 1

    def kernel(ids, q_ref, jac_ref, recv_ref, mid_ref, left_ref, right_ref, up_ref, down_ref,
               up_right_ref, down_left_ref, out_ref, win_ref, spread_ref):
        row_id = ids[0]
        col_id = ids[1]
        first_row = row_id * tile_rows
        low_slot = col_id * band_local - 2
        low_offset = col_id * band_local - half_band
        size = jac_ref.shape[-1]

        for col_value in range(col_count):
            offset = col_value * band_local - half_band

            @pl.when(col_id == col_value)
            def _():
                for position in range(window):
                    at = offset + position
                    for g in range(3):
                        if at < 0:
                            win_ref[position, g] = recv_ref[sent_rows + at, g]
                        elif at < tile_rows:
                            win_ref[position, g] = jac_ref[at, g]
                        else:
                            win_ref[position, g] = recv_ref[at - tile_rows, g]

        def prior_tile(ext_row, ext_slot, masked):
            if ext_slot < 2:
                if ext_row == tile_rows + 1:
                    tile = down_left_ref[band_local - 2 + ext_slot]
                else:
                    tile = left_ref[ext_row - 1, band_local - 2 + ext_slot]
            elif ext_slot >= 2 + band_local:
                if ext_row == 0:
                    tile = up_right_ref[ext_slot - 2 - band_local]
                else:
                    tile = right_ref[ext_row - 1, ext_slot - 2 - band_local]
            elif ext_row == 0:
                tile = up_ref[ext_slot - 2]
            elif ext_row == tile_rows + 1:
                tile = down_ref[ext_slot - 2]
            else:
                tile = mid_ref[ext_row - 1, ext_slot - 2]
            if not masked:
                return tile
            column = first_row + ext_row - 1 + low_slot + ext_slot - half_band
            keep = (column >= 0) & (column < grid_tiles)
            return jnp.where(keep, tile, jnp.zeros_like(tile))

        eye = lax.broadcasted_iota(jnp.int32, (size, size), 0) == lax.broadcasted_iota(
            jnp.int32, (size, size), 1
        )

        def body(masked):
            for row in range(tile_rows):
                lhs = jnp.concatenate([jac_ref[row, f] for f in range(3)], axis=1)
                rhs = jnp.concatenate(
                    [
                        jnp.concatenate(
                            [prior_tile(row + f, u - f + 2, masked) for u in range(extended)], axis=1
                        )
                        for f in range(3)
                    ],
                    axis=0,
                )
                spread_ref[row] = jnp.dot(lhs, rhs, preferred_element_type=jnp.float32).astype(
                    jnp.bfloat16
                )
            for position in range(window):
                members = [
                    (position - k, k) for k in range(band_local) if 0 <= position - k < tile_rows
                ]
                left_side = jnp.concatenate(
                    [spread_ref[row, :, k * size : (k + 3) * size] for row, k in members], axis=0
                )
                right_side = jnp.concatenate([win_ref[position, g] for g in range(3)], axis=1)
                product = lax.dot_general(
                    left_side,
                    right_side,
                    (((1,), (1,)), ((), ())),
                    preferred_element_type=jnp.float32,
                )
                for index, (row, k) in enumerate(members):
                    total = product[index * size : (index + 1) * size]
                    on_diagonal = (low_offset + k == 0).astype(jnp.float32)
                    noise = jnp.where(eye, q_ref[pl.ds(row, 1), :], 0.0)
                    total = total + noise * on_diagonal
                    if masked:
                        column = first_row + row + low_offset + k
                        keep = (column >= 0) & (column < grid_tiles)
                        total = jnp.where(keep, total, jnp.zeros_like(total))
                    out_ref[row, k] = total.astype(out_ref.dtype)

        edge = (row_id == 0) | (row_id == row_count - 1)

        @pl.when(edge)
        def _():
            body(True)

        @pl.when(jnp.logical_not(edge))
        def _():
            body(False)

    return kernel


def shards(p_band, blocks, block_offsets, block_live, q_var):
    tile_rows, band_local, tile_size = p_band.shape[0], p_band.shape[1], p_band.shape[2]
    row_count = lax.axis_size("row")
    col_count = lax.axis_size("col")
    half_band = band_local * col_count // 2
    grid_tiles = tile_rows * row_count
    row_id = lax.axis_index("row")
    col_id = lax.axis_index("col")
    low_offset = col_id * band_local - half_band

    def flat(a, b):
        return a * col_count + b

    left = lax.ppermute(p_band, "col", [(b, b + 1) for b in range(col_count - 1)])
    right = lax.ppermute(p_band, "col", [(b + 1, b) for b in range(col_count - 1)])

    sent_rows = half_band
    lower_half = col_id < col_count // 2
    send_start = jnp.where(lower_half, tile_rows - sent_rows, 0)
    sent_offsets = lax.dynamic_slice_in_dim(block_offsets, send_start, sent_rows, 0)
    sent_live = lax.dynamic_slice_in_dim(block_live, send_start, sent_rows, 0)
    meta = jnp.zeros((tile_size, tile_size), blocks.dtype)
    meta = meta.at[0, : sent_rows * 3].set(sent_offsets.reshape(-1).astype(blocks.dtype))
    meta = meta.at[1, :sent_rows].set(sent_live.astype(blocks.dtype))
    sent_tiles = lax.dynamic_slice_in_dim(blocks, send_start, sent_rows, 0).reshape(
        (sent_rows * 3, tile_size, tile_size)
    )
    with_rows = lax.dynamic_slice_in_dim(p_band, jnp.where(lower_half, tile_rows - 1, 0), 1, 0)[0]
    alone_rows = lax.dynamic_slice_in_dim(p_band, jnp.where(lower_half, 0, tile_rows - 1), 1, 0)[0]
    sent = jnp.concatenate([sent_tiles, meta[None], with_rows], axis=0)
    pairs = []
    for b in range(col_count):
        if b * band_local - half_band < 0:
            pairs += [(flat(a, b), flat(a + 1, b)) for a in range(row_count - 1)]
        else:
            pairs += [(flat(a, b), flat(a - 1, b)) for a in range(1, row_count)]
    received_all = lax.ppermute(sent, ("row", "col"), pairs)
    received_alone = lax.ppermute(alone_rows, ("row", "col"), [(t, f) for f, t in pairs])
    received_with = received_all[sent_rows * 3 + 1 :]
    up = jnp.where(lower_half, received_with, received_alone)
    down = jnp.where(lower_half, received_alone, received_with)

    jacobian = assemble(blocks, block_offsets, block_live)
    received_meta = received_all[sent_rows * 3].astype(jnp.float32)
    received = assemble(
        received_all[: sent_rows * 3].reshape((sent_rows, 3, tile_size, tile_size)),
        jnp.round(received_meta[0, : sent_rows * 3]).astype(jnp.int32).reshape(sent_rows, 3),
        jnp.round(received_meta[1, :sent_rows]).astype(jnp.int32),
    )

    down_left = lax.ppermute(down, "col", [(b, b + 1) for b in range(col_count - 1)])
    up_right = lax.ppermute(up, "col", [(b + 1, b) for b in range(col_count - 1)])

    ids = jnp.stack([row_id, col_id]).astype(jnp.int32)
    vmem = pl.BlockSpec(memory_space=pltpu.MemorySpace.VMEM)
    smem = pl.BlockSpec(memory_space=pltpu.MemorySpace.SMEM)
    return pl.pallas_call(
        band_kernel(tile_rows, band_local, half_band, grid_tiles, sent_rows, row_count, col_count),
        out_shape=jax.ShapeDtypeStruct(p_band.shape, p_band.dtype),
        in_specs=[smem] + [vmem] * 10,
        out_specs=vmem,
        scratch_shapes=[
            pltpu.VMEM((tile_rows + band_local - 1, 3, tile_size, tile_size), p_band.dtype),
            pltpu.VMEM((tile_rows, tile_size, (band_local + 2) * tile_size), p_band.dtype),
        ],
    )(ids, q_var, jacobian, received, p_band, left, right, up, down, up_right, down_left)


def solution(mesh):
    placed = (
        P("row", "col", None, None),
        P("row", None, None, None),
        P("row", None),
        P("row"),
        P("row", None),
    )
    return jax.shard_map(
        shards, mesh=mesh, in_specs=placed, out_specs=P("row", "col", None, None), check_vma=False
    )
```

```python
import jax
import jax.numpy as jnp
from jax import lax
from jax.experimental import pallas as pl
from jax.experimental.pallas import tpu as pltpu
from jax.sharding import PartitionSpec as P


def assemble(blocks, block_offsets, block_live):
    slot_ids = jnp.arange(blocks.shape[1], dtype=jnp.int32)
    alive = slot_ids[None, :] < block_live[:, None]
    pieces = []
    for target in (-1, 0, 1):
        choose = (block_offsets == target) & alive
        total = jnp.zeros(blocks.shape[:1] + blocks.shape[2:], jnp.float32)
        for m in range(blocks.shape[1]):
            total = total + jnp.where(choose[:, m, None, None], blocks[:, m].astype(jnp.float32), 0.0)
        pieces.append(total.astype(jnp.bfloat16))
    return jnp.stack(pieces, axis=1)


def band_kernel(tile_rows, band_local, half_band, grid_tiles, sent_rows, row_count, col_count):
    extended = band_local + 2
    window = tile_rows + band_local - 1

    def kernel(ids, q_ref, jac_ref, recv_ref, mid_ref, left_ref, right_ref, up_ref, down_ref,
               up_right_ref, down_left_ref, out_ref, win_ref, spread_ref):
        row_id = ids[0]
        col_id = ids[1]
        first_row = row_id * tile_rows
        low_slot = col_id * band_local - 2
        low_offset = col_id * band_local - half_band
        size = jac_ref.shape[-1]

        for col_value in range(col_count):
            offset = col_value * band_local - half_band

            @pl.when(col_id == col_value)
            def _():
                for position in range(window):
                    at = offset + position
                    for g in range(3):
                        if at < 0:
                            win_ref[position, g] = recv_ref[sent_rows + at, g]
                        elif at < tile_rows:
                            win_ref[position, g] = jac_ref[at, g]
                        else:
                            win_ref[position, g] = recv_ref[at - tile_rows, g]

        def prior_tile(ext_row, ext_slot, masked):
            if ext_slot < 2:
                if ext_row == tile_rows + 1:
                    tile = down_left_ref[band_local - 2 + ext_slot]
                else:
                    tile = left_ref[(ext_row - 1) * band_local + band_local - 2 + ext_slot - 1]
            elif ext_slot >= 2 + band_local:
                if ext_row == 0:
                    tile = up_right_ref[ext_slot - 2 - band_local]
                else:
                    tile = right_ref[(ext_row - 1) * band_local + ext_slot - 2 - band_local]
            elif ext_row == 0:
                tile = up_ref[ext_slot - 2]
            elif ext_row == tile_rows + 1:
                tile = down_ref[ext_slot - 2]
            else:
                tile = mid_ref[ext_row - 1, ext_slot - 2]
            if not masked:
                return tile
            column = first_row + ext_row - 1 + low_slot + ext_slot - half_band
            keep = (column >= 0) & (column < grid_tiles)
            return jnp.where(keep, tile, jnp.zeros_like(tile))

        eye = lax.broadcasted_iota(jnp.int32, (size, size), 0) == lax.broadcasted_iota(
            jnp.int32, (size, size), 1
        )

        def body(masked):
            for row in range(tile_rows):
                lhs = jnp.concatenate([jac_ref[row, f] for f in range(3)], axis=1)
                rhs = jnp.concatenate(
                    [
                        jnp.concatenate(
                            [prior_tile(row + f, u - f + 2, masked) for u in range(extended)], axis=1
                        )
                        for f in range(3)
                    ],
                    axis=0,
                )
                spread_ref[row] = jnp.dot(lhs, rhs, preferred_element_type=jnp.float32).astype(
                    jnp.bfloat16
                )
            for position in range(window):
                members = [
                    (position - k, k) for k in range(band_local) if 0 <= position - k < tile_rows
                ]
                left_side = jnp.concatenate(
                    [spread_ref[row, :, k * size : (k + 3) * size] for row, k in members], axis=0
                )
                right_side = jnp.concatenate([win_ref[position, g] for g in range(3)], axis=1)
                product = lax.dot_general(
                    left_side,
                    right_side,
                    (((1,), (1,)), ((), ())),
                    preferred_element_type=jnp.float32,
                )
                for index, (row, k) in enumerate(members):
                    total = product[index * size : (index + 1) * size]
                    on_diagonal = (low_offset + k == 0).astype(jnp.float32)
                    noise = jnp.where(eye, q_ref[pl.ds(row, 1), :], 0.0)
                    total = total + noise * on_diagonal
                    if masked:
                        column = first_row + row + low_offset + k
                        keep = (column >= 0) & (column < grid_tiles)
                        total = jnp.where(keep, total, jnp.zeros_like(total))
                    out_ref[row, k] = total.astype(out_ref.dtype)

        edge = (row_id == 0) | (row_id == row_count - 1)

        @pl.when(edge)
        def _():
            body(True)

        @pl.when(jnp.logical_not(edge))
        def _():
            body(False)

    return kernel


def shards(p_band, blocks, block_offsets, block_live, q_var):
    tile_rows, band_local, tile_size = p_band.shape[0], p_band.shape[1], p_band.shape[2]
    row_count = lax.axis_size("row")
    col_count = lax.axis_size("col")
    half_band = band_local * col_count // 2
    grid_tiles = tile_rows * row_count
    row_id = lax.axis_index("row")
    col_id = lax.axis_index("col")
    low_offset = col_id * band_local - half_band

    def flat(a, b):
        return a * col_count + b

    flat_band = p_band.reshape((tile_rows * band_local, tile_size, tile_size))
    left = lax.ppermute(flat_band[1:], "col", [(b, b + 1) for b in range(col_count - 1)])
    right = lax.ppermute(flat_band[:-1], "col", [(b + 1, b) for b in range(col_count - 1)])
    up = lax.ppermute(p_band[-1], "row", [(a, a + 1) for a in range(row_count - 1)])
    down = lax.ppermute(p_band[0], "row", [(a + 1, a) for a in range(row_count - 1)])

    sent_rows = half_band
    lower_half = col_id < col_count // 2
    send_start = jnp.where(lower_half, tile_rows - sent_rows, 0)
    sent_offsets = lax.dynamic_slice_in_dim(block_offsets, send_start, sent_rows, 0)
    sent_live = lax.dynamic_slice_in_dim(block_live, send_start, sent_rows, 0)
    meta = jnp.zeros((tile_size, tile_size), blocks.dtype)
    meta = meta.at[0, : sent_rows * 3].set(sent_offsets.reshape(-1).astype(blocks.dtype))
    meta = meta.at[1, :sent_rows].set(sent_live.astype(blocks.dtype))
    sent_tiles = lax.dynamic_slice_in_dim(blocks, send_start, sent_rows, 0).reshape(
        (sent_rows * 3, tile_size, tile_size)
    )
    sent = jnp.concatenate([sent_tiles, meta[None]], axis=0)
    pairs = []
    for b in range(col_count):
        if b * band_local - half_band < 0:
            pairs += [(flat(a, b), flat(a + 1, b)) for a in range(row_count - 1)]
        else:
            pairs += [(flat(a, b), flat(a - 1, b)) for a in range(1, row_count)]
    received_all = lax.ppermute(sent, ("row", "col"), pairs)

    jacobian = assemble(blocks, block_offsets, block_live)
    received_meta = received_all[sent_rows * 3].astype(jnp.float32)
    received = assemble(
        received_all[: sent_rows * 3].reshape((sent_rows, 3, tile_size, tile_size)),
        jnp.round(received_meta[0, : sent_rows * 3]).astype(jnp.int32).reshape(sent_rows, 3),
        jnp.round(received_meta[1, :sent_rows]).astype(jnp.int32),
    )

    down_left = lax.ppermute(down, "col", [(b, b + 1) for b in range(col_count - 1)])
    up_right = lax.ppermute(up, "col", [(b + 1, b) for b in range(col_count - 1)])

    ids = jnp.stack([row_id, col_id]).astype(jnp.int32)
    vmem = pl.BlockSpec(memory_space=pltpu.MemorySpace.VMEM)
    smem = pl.BlockSpec(memory_space=pltpu.MemorySpace.SMEM)
    return pl.pallas_call(
        band_kernel(tile_rows, band_local, half_band, grid_tiles, sent_rows, row_count, col_count),
        out_shape=jax.ShapeDtypeStruct(p_band.shape, p_band.dtype),
        in_specs=[smem] + [vmem] * 10,
        out_specs=vmem,
        scratch_shapes=[
            pltpu.VMEM((tile_rows + band_local - 1, 3, tile_size, tile_size), p_band.dtype),
            pltpu.VMEM((tile_rows, tile_size, (band_local + 2) * tile_size), p_band.dtype),
        ],
    )(ids, q_var, jacobian, received, p_band, left, right, up, down, up_right, down_left)


def solution(mesh):
    placed = (
        P("row", "col", None, None),
        P("row", None, None, None),
        P("row", None),
        P("row"),
        P("row", None),
    )
    return jax.shard_map(
        shards, mesh=mesh, in_specs=placed, out_specs=P("row", "col", None, None), check_vma=False
    )
```

```python
import jax
import jax.numpy as jnp
from jax import lax
from jax.experimental import pallas as pl
from jax.experimental.pallas import tpu as pltpu
from jax.sharding import PartitionSpec as P


def assemble(blocks, block_offsets, block_live):
    slot_ids = jnp.arange(blocks.shape[1], dtype=jnp.int32)
    alive = slot_ids[None, :] < block_live[:, None]
    pieces = []
    for target in (-1, 0, 1):
        choose = (block_offsets == target) & alive
        total = jnp.zeros(blocks.shape[:1] + blocks.shape[2:], jnp.float32)
        for m in range(blocks.shape[1]):
            total = total + jnp.where(choose[:, m, None, None], blocks[:, m].astype(jnp.float32), 0.0)
        pieces.append(total.astype(jnp.bfloat16))
    return jnp.stack(pieces, axis=1)


def band_kernel(tile_rows, band_local, half_band, grid_tiles, sent_rows, row_count, col_count):
    extended = band_local + 2
    window = tile_rows + band_local - 1

    def kernel(ids, q_ref, jac_ref, recv_ref, mid_ref, left_ref, right_ref, up_ref, down_ref,
               up_right_ref, down_left_ref, out_ref, win_ref, spread_ref):
        row_id = ids[0]
        col_id = ids[1]
        first_row = row_id * tile_rows
        low_slot = col_id * band_local - 2
        low_offset = col_id * band_local - half_band
        size = jac_ref.shape[-1]

        for col_value in range(col_count):
            offset = col_value * band_local - half_band

            @pl.when(col_id == col_value)
            def _():
                for position in range(window):
                    at = offset + position
                    for g in range(3):
                        if at < 0:
                            win_ref[position, g] = recv_ref[sent_rows + at, g]
                        elif at < tile_rows:
                            win_ref[position, g] = jac_ref[at, g]
                        else:
                            win_ref[position, g] = recv_ref[at - tile_rows, g]

        def prior_tile(ext_row, ext_slot, masked):
            if ext_slot < 2:
                if ext_row == tile_rows + 1:
                    tile = down_left_ref[band_local - 2 + ext_slot]
                else:
                    tile = left_ref[ext_row - 1, band_local - 2 + ext_slot]
            elif ext_slot >= 2 + band_local:
                if ext_row == 0:
                    tile = up_right_ref[ext_slot - 2 - band_local]
                else:
                    tile = right_ref[ext_row - 1, ext_slot - 2 - band_local]
            elif ext_row == 0:
                tile = up_ref[ext_slot - 2]
            elif ext_row == tile_rows + 1:
                tile = down_ref[ext_slot - 2]
            else:
                tile = mid_ref[ext_row - 1, ext_slot - 2]
            if not masked:
                return tile
            column = first_row + ext_row - 1 + low_slot + ext_slot - half_band
            keep = (column >= 0) & (column < grid_tiles)
            return jnp.where(keep, tile, jnp.zeros_like(tile))

        eye = lax.broadcasted_iota(jnp.int32, (size, size), 0) == lax.broadcasted_iota(
            jnp.int32, (size, size), 1
        )

        def body(masked):
            for row in range(tile_rows):
                acc = None
                for f in range(3):
                    slab = jnp.concatenate(
                        [prior_tile(row + f, u - f + 2, masked) for u in range(extended)], axis=1
                    )
                    term = jnp.dot(jac_ref[row, f], slab, preferred_element_type=jnp.float32)
                    acc = term if acc is None else acc + term
                spread_ref[row] = acc.astype(jnp.bfloat16)
            for position in range(window):
                members = [
                    (position - k, k) for k in range(band_local) if 0 <= position - k < tile_rows
                ]
                left_side = jnp.concatenate(
                    [spread_ref[row, :, k * size : (k + 3) * size] for row, k in members], axis=0
                )
                right_side = jnp.concatenate([win_ref[position, g] for g in range(3)], axis=1)
                product = lax.dot_general(
                    left_side,
                    right_side,
                    (((1,), (1,)), ((), ())),
                    preferred_element_type=jnp.float32,
                )
                for index, (row, k) in enumerate(members):
                    total = product[index * size : (index + 1) * size]
                    on_diagonal = (low_offset + k == 0).astype(jnp.float32)
                    noise = jnp.where(eye, q_ref[pl.ds(row, 1), :], 0.0)
                    total = total + noise * on_diagonal
                    if masked:
                        column = first_row + row + low_offset + k
                        keep = (column >= 0) & (column < grid_tiles)
                        total = jnp.where(keep, total, jnp.zeros_like(total))
                    out_ref[row, k] = total.astype(out_ref.dtype)

        edge = (row_id == 0) | (row_id == row_count - 1)

        @pl.when(edge)
        def _():
            body(True)

        @pl.when(jnp.logical_not(edge))
        def _():
            body(False)

    return kernel


def shards(p_band, blocks, block_offsets, block_live, q_var):
    tile_rows, band_local, tile_size = p_band.shape[0], p_band.shape[1], p_band.shape[2]
    row_count = lax.axis_size("row")
    col_count = lax.axis_size("col")
    half_band = band_local * col_count // 2
    grid_tiles = tile_rows * row_count
    row_id = lax.axis_index("row")
    col_id = lax.axis_index("col")
    low_offset = col_id * band_local - half_band

    def flat(a, b):
        return a * col_count + b

    left = lax.ppermute(p_band, "col", [(b, b + 1) for b in range(col_count - 1)])
    right = lax.ppermute(p_band, "col", [(b + 1, b) for b in range(col_count - 1)])
    up = lax.ppermute(p_band[-1], "row", [(a, a + 1) for a in range(row_count - 1)])
    down = lax.ppermute(p_band[0], "row", [(a + 1, a) for a in range(row_count - 1)])

    sent_rows = half_band
    lower_half = col_id < col_count // 2
    send_start = jnp.where(lower_half, tile_rows - sent_rows, 0)
    sent_offsets = lax.dynamic_slice_in_dim(block_offsets, send_start, sent_rows, 0)
    sent_live = lax.dynamic_slice_in_dim(block_live, send_start, sent_rows, 0)
    meta = jnp.zeros((tile_size, tile_size), blocks.dtype)
    meta = meta.at[0, : sent_rows * 3].set(sent_offsets.reshape(-1).astype(blocks.dtype))
    meta = meta.at[1, :sent_rows].set(sent_live.astype(blocks.dtype))
    sent_tiles = lax.dynamic_slice_in_dim(blocks, send_start, sent_rows, 0).reshape(
        (sent_rows * 3, tile_size, tile_size)
    )
    sent = jnp.concatenate([sent_tiles, meta[None]], axis=0)
    pairs = []
    for b in range(col_count):
        if b * band_local - half_band < 0:
            pairs += [(flat(a, b), flat(a + 1, b)) for a in range(row_count - 1)]
        else:
            pairs += [(flat(a, b), flat(a - 1, b)) for a in range(1, row_count)]
    received_all = lax.ppermute(sent, ("row", "col"), pairs)

    jacobian = assemble(blocks, block_offsets, block_live)
    received_meta = received_all[sent_rows * 3].astype(jnp.float32)
    received = assemble(
        received_all[: sent_rows * 3].reshape((sent_rows, 3, tile_size, tile_size)),
        jnp.round(received_meta[0, : sent_rows * 3]).astype(jnp.int32).reshape(sent_rows, 3),
        jnp.round(received_meta[1, :sent_rows]).astype(jnp.int32),
    )

    down_left = lax.ppermute(down, "col", [(b, b + 1) for b in range(col_count - 1)])
    up_right = lax.ppermute(up, "col", [(b + 1, b) for b in range(col_count - 1)])

    ids = jnp.stack([row_id, col_id]).astype(jnp.int32)
    vmem = pl.BlockSpec(memory_space=pltpu.MemorySpace.VMEM)
    smem = pl.BlockSpec(memory_space=pltpu.MemorySpace.SMEM)
    return pl.pallas_call(
        band_kernel(tile_rows, band_local, half_band, grid_tiles, sent_rows, row_count, col_count),
        out_shape=jax.ShapeDtypeStruct(p_band.shape, p_band.dtype),
        in_specs=[smem] + [vmem] * 10,
        out_specs=vmem,
        scratch_shapes=[
            pltpu.VMEM((tile_rows + band_local - 1, 3, tile_size, tile_size), p_band.dtype),
            pltpu.VMEM((tile_rows, tile_size, (band_local + 2) * tile_size), p_band.dtype),
        ],
    )(ids, q_var, jacobian, received, p_band, left, right, up, down, up_right, down_left)


def solution(mesh):
    placed = (
        P("row", "col", None, None),
        P("row", None, None, None),
        P("row", None),
        P("row"),
        P("row", None),
    )
    return jax.shard_map(
        shards, mesh=mesh, in_specs=placed, out_specs=P("row", "col", None, None), check_vma=False
    )
```

```python
import jax
import jax.numpy as jnp
from jax import lax
from jax.experimental import pallas as pl
from jax.experimental.pallas import tpu as pltpu
from jax.sharding import PartitionSpec as P


def assemble(blocks, block_offsets, block_live):
    slot_ids = jnp.arange(blocks.shape[1], dtype=jnp.int32)
    alive = slot_ids[None, :] < block_live[:, None]
    pieces = []
    for target in (-1, 0, 1):
        choose = (block_offsets == target) & alive
        total = jnp.zeros(blocks.shape[:1] + blocks.shape[2:], jnp.float32)
        for m in range(blocks.shape[1]):
            total = total + jnp.where(choose[:, m, None, None], blocks[:, m].astype(jnp.float32), 0.0)
        pieces.append(total.astype(jnp.bfloat16))
    return jnp.stack(pieces, axis=1)


def band_kernel(tile_rows, band_local, half_band, grid_tiles, sent_rows, row_count, col_count):
    extended = band_local + 2
    window = tile_rows + band_local - 1

    def kernel(ids, q_ref, jac_ref, recv_ref, mid_ref, left_ref, right_ref, up_ref, down_ref,
               up_right_ref, down_left_ref, out_ref, win_ref, spread_ref):
        row_id = ids[0]
        col_id = ids[1]
        first_row = row_id * tile_rows
        low_slot = col_id * band_local - 2
        low_offset = col_id * band_local - half_band
        size = jac_ref.shape[-1]

        def received_tile(row, g):
            total = jnp.zeros((size, size), jnp.float32)
            for m in range(3):
                pick = (ids[2 + row * 3 + m] == g - 1) & (m < ids[2 + sent_rows * 3 + row])
                block = recv_ref[row * 3 + m].astype(jnp.float32)
                total = total + jnp.where(pick, block, 0.0)
            return total.astype(win_ref.dtype)

        for col_value in range(col_count):
            offset = col_value * band_local - half_band

            @pl.when(col_id == col_value)
            def _():
                for position in range(window):
                    at = offset + position
                    for g in range(3):
                        if 0 <= at < tile_rows:
                            win_ref[position, g] = jac_ref[at, g]
                        else:
                            win_ref[position, g] = received_tile(
                                sent_rows + at if at < 0 else at - tile_rows, g
                            )

        def prior_tile(ext_row, ext_slot, masked):
            if ext_slot < 2:
                if ext_row == tile_rows + 1:
                    tile = down_left_ref[band_local - 2 + ext_slot]
                else:
                    tile = left_ref[ext_row - 1, band_local - 2 + ext_slot]
            elif ext_slot >= 2 + band_local:
                if ext_row == 0:
                    tile = up_right_ref[ext_slot - 2 - band_local]
                else:
                    tile = right_ref[ext_row - 1, ext_slot - 2 - band_local]
            elif ext_row == 0:
                tile = up_ref[ext_slot - 2]
            elif ext_row == tile_rows + 1:
                tile = down_ref[ext_slot - 2]
            else:
                tile = mid_ref[ext_row - 1, ext_slot - 2]
            if not masked:
                return tile
            column = first_row + ext_row - 1 + low_slot + ext_slot - half_band
            keep = (column >= 0) & (column < grid_tiles)
            return jnp.where(keep, tile, jnp.zeros_like(tile))

        eye = lax.broadcasted_iota(jnp.int32, (size, size), 0) == lax.broadcasted_iota(
            jnp.int32, (size, size), 1
        )

        def body(masked):
            for row in range(tile_rows):
                lhs = jnp.concatenate([jac_ref[row, f] for f in range(3)], axis=1)
                rhs = jnp.concatenate(
                    [
                        jnp.concatenate(
                            [prior_tile(row + f, u - f + 2, masked) for u in range(extended)], axis=1
                        )
                        for f in range(3)
                    ],
                    axis=0,
                )
                spread_ref[row] = jnp.dot(lhs, rhs, preferred_element_type=jnp.float32).astype(
                    jnp.bfloat16
                )
            for position in range(window):
                members = [
                    (position - k, k) for k in range(band_local) if 0 <= position - k < tile_rows
                ]
                left_side = jnp.concatenate(
                    [spread_ref[row, :, k * size : (k + 3) * size] for row, k in members], axis=0
                )
                right_side = jnp.concatenate([win_ref[position, g] for g in range(3)], axis=1)
                product = lax.dot_general(
                    left_side,
                    right_side,
                    (((1,), (1,)), ((), ())),
                    preferred_element_type=jnp.float32,
                )
                for index, (row, k) in enumerate(members):
                    total = product[index * size : (index + 1) * size]
                    on_diagonal = (low_offset + k == 0).astype(jnp.float32)
                    noise = jnp.where(eye, q_ref[pl.ds(row, 1), :], 0.0)
                    total = total + noise * on_diagonal
                    if masked:
                        column = first_row + row + low_offset + k
                        keep = (column >= 0) & (column < grid_tiles)
                        total = jnp.where(keep, total, jnp.zeros_like(total))
                    out_ref[row, k] = total.astype(out_ref.dtype)

        edge = (row_id == 0) | (row_id == row_count - 1)

        @pl.when(edge)
        def _():
            body(True)

        @pl.when(jnp.logical_not(edge))
        def _():
            body(False)

    return kernel


def shards(p_band, blocks, block_offsets, block_live, q_var):
    tile_rows, band_local, tile_size = p_band.shape[0], p_band.shape[1], p_band.shape[2]
    row_count = lax.axis_size("row")
    col_count = lax.axis_size("col")
    half_band = band_local * col_count // 2
    grid_tiles = tile_rows * row_count
    row_id = lax.axis_index("row")
    col_id = lax.axis_index("col")
    low_offset = col_id * band_local - half_band

    def flat(a, b):
        return a * col_count + b

    left = lax.ppermute(p_band, "col", [(b, b + 1) for b in range(col_count - 1)])
    right = lax.ppermute(p_band, "col", [(b + 1, b) for b in range(col_count - 1)])
    up = lax.ppermute(p_band[-1], "row", [(a, a + 1) for a in range(row_count - 1)])
    down = lax.ppermute(p_band[0], "row", [(a + 1, a) for a in range(row_count - 1)])

    sent_rows = half_band
    lower_half = col_id < col_count // 2
    send_start = jnp.where(lower_half, tile_rows - sent_rows, 0)
    sent_offsets = lax.dynamic_slice_in_dim(block_offsets, send_start, sent_rows, 0)
    sent_live = lax.dynamic_slice_in_dim(block_live, send_start, sent_rows, 0)
    meta = jnp.zeros((tile_size, tile_size), blocks.dtype)
    meta = meta.at[0, : sent_rows * 3].set(sent_offsets.reshape(-1).astype(blocks.dtype))
    meta = meta.at[1, :sent_rows].set(sent_live.astype(blocks.dtype))
    sent_tiles = lax.dynamic_slice_in_dim(blocks, send_start, sent_rows, 0).reshape(
        (sent_rows * 3, tile_size, tile_size)
    )
    sent = jnp.concatenate([sent_tiles, meta[None]], axis=0)
    pairs = []
    for b in range(col_count):
        if b * band_local - half_band < 0:
            pairs += [(flat(a, b), flat(a + 1, b)) for a in range(row_count - 1)]
        else:
            pairs += [(flat(a, b), flat(a - 1, b)) for a in range(1, row_count)]
    received_all = lax.ppermute(sent, ("row", "col"), pairs)

    jacobian = assemble(blocks, block_offsets, block_live)
    received_meta = received_all[sent_rows * 3].astype(jnp.float32)
    received_ints = jnp.round(received_meta[0:2]).astype(jnp.int32)

    down_left = lax.ppermute(down, "col", [(b, b + 1) for b in range(col_count - 1)])
    up_right = lax.ppermute(up, "col", [(b + 1, b) for b in range(col_count - 1)])

    ids = jnp.concatenate(
        [
            jnp.stack([row_id, col_id]).astype(jnp.int32),
            received_ints[0, : sent_rows * 3],
            received_ints[1, :sent_rows],
        ]
    )
    vmem = pl.BlockSpec(memory_space=pltpu.MemorySpace.VMEM)
    smem = pl.BlockSpec(memory_space=pltpu.MemorySpace.SMEM)
    return pl.pallas_call(
        band_kernel(tile_rows, band_local, half_band, grid_tiles, sent_rows, row_count, col_count),
        out_shape=jax.ShapeDtypeStruct(p_band.shape, p_band.dtype),
        in_specs=[smem] + [vmem] * 10,
        out_specs=vmem,
        scratch_shapes=[
            pltpu.VMEM((tile_rows + band_local - 1, 3, tile_size, tile_size), p_band.dtype),
            pltpu.VMEM((tile_rows, tile_size, (band_local + 2) * tile_size), p_band.dtype),
        ],
    )(ids, q_var, jacobian, received_all, p_band, left, right, up, down, up_right, down_left)


def solution(mesh):
    placed = (
        P("row", "col", None, None),
        P("row", None, None, None),
        P("row", None),
        P("row"),
        P("row", None),
    )
    return jax.shard_map(
        shards, mesh=mesh, in_specs=placed, out_specs=P("row", "col", None, None), check_vma=False
    )
```
